32 devices in a mesh: dom: 8 (over z, core), cls: 4 (over y, x).
Axes of the slice: x: 2, y: 2, z: 4, core: 2. Of those that a mesh axis runs over, the one named last changes fastest.
Arguments:
- particles: bfloat16 [8192, 9216], P('dom'), may hold values from -6 to 6
- defocus: float32 [8192], P('dom'), may hold values from 0.5 to 2
- inv_noise: float32 [4608], replicated, may hold values from 0.25 to 4
- references: bfloat16 [96, 8, 9216], P(('cls', 'dom')), may hold values from -0.125 to 0.125
- part_class: int32 [8192], P('dom'), may hold values from 0 to 95, as said below
- part_rot: int32 [8192], P('dom'), may hold values from 0 to 7
- counts: int32 [96], replicated, may hold values from 0 to 399
Outputs:
- best_score: float32 [8192], P('dom')
- class_images: float32 [96, 8, 9216], P(('cls', 'dom'))
The draws below stay inside these ranges and needn't reach their ends.
Inputs may be any that keep to these rules, and one draw needn't show every extreme that they name: `part_class`: block o of classes is o * 3 to o * 3 + 2. In each aligned block of 1024 particles at most 96 have their class in any one block of classes; in every draw one block of classes receives exactly 96 from every block of particles.
All inputs are finite; a program needn't handle non-finite values.
Results may differ from the reference program's by a relative error of at most 0.0044.
Values may be sent and summed in bfloat16 or wider, within the bound.
No kernel may reach another device: no remote copies, remote signals or barrier semaphores. Data moves between devices by JAX's collectives and lax.ppermute only.
A program may use at most 192 MiB of HBM per device.

```python
import math
import jax
import jax.numpy as jnp
from jax import lax

PIX = 4608
R = 8
K_DEV = 3
PART_DEV = 1024
K = 96
PARTICLES = 8192
CAP = 96


def draw_part_class(key, part):
    owners = K // K_DEV
    blocks = PARTICLES // PART_DEV
    key_busy, key_blocks = jax.random.split(jax.random.fold_in(key, 17))
    busiest = jax.random.randint(key_busy, (), 0, owners)

    def draw_block(block_key):
        first_key, second_key, third_key = jax.random.split(block_key, 3)
        slot_order = jax.random.permutation(first_key, (owners - 1) * CAP)[:PART_DEV - CAP]
        others = (slot_order // CAP).astype(jnp.int32)
        others = others + (others >= busiest).astype(jnp.int32)
        owner_ids = jnp.concatenate([jnp.full((CAP,), busiest, jnp.int32), others])
        owner_ids = jax.random.permutation(second_key, owner_ids)
        within = jax.random.randint(third_key, (PART_DEV,), 0, K_DEV)
        return (owner_ids * K_DEV + within).astype(jnp.int32)
    block_keys = jax.random.split(key_blocks, blocks)
    return jax.vmap(draw_block)(block_keys).reshape(PARTICLES)


def set_ends(entries, stream_key, low, high):
    dims = entries.shape
    index_at = [jax.random.randint(jax.random.fold_in(stream_key, axis), (), 0, dims[axis]) for axis in range(len(dims))]
    entries = entries.at[tuple(index_at)].set(low)
    longest = dims.index(max(dims))
    index_at[longest] = (index_at[longest] + 1) % dims[longest]
    return entries.at[tuple(index_at)].set(high)


def shard_levels(own_key, extent, pieces, least, top_value):
    def one(dim, parts):
        draws = jax.random.uniform(jax.random.fold_in(jax.random.fold_in(own_key, 6), dim), (parts,), jnp.float32, least / len(pieces), top_value / len(pieces))
        return jnp.repeat(jnp.exp(draws), extent[dim] // parts).reshape((-1,) + (1,) * (len(extent) - dim - 1))

    level = one(*pieces[0])
    for cut in pieces[1:]:
        level = level * one(*cut)
    return level


def bell_draw(key, extent, spread, most, shards=(), kind=jnp.bfloat16):
    level = shard_levels(key, extent, shards, -0.22, 0.18) if shards else 1.0
    entries = jax.random.normal(key, extent, jnp.float32) * spread * level
    return jnp.minimum(jnp.maximum(entries, -most), most).astype(kind)


def setup_inputs(seed: int = 0) -> dict:
    streams_of = jax.random.split(jax.random.key(seed), 8)
    particles = bell_draw(streams_of[0], (PARTICLES, 2 * PIX), 1.0, 6.0, ((0, 8),))
    defocus = jnp.clip(0.5 + 1.5 * jax.random.uniform(streams_of[1], (PARTICLES,), jnp.float32) ** shard_levels(streams_of[1], (PARTICLES,), ((0, 8),), -0.2, 0.2), 0.5, 2.0)
    inv_noise = jnp.clip(jnp.exp(jax.random.uniform(streams_of[2], (PIX,), jnp.float32, math.log(0.25), math.log(4.0))), 0.25, 4.0)
    references = bell_draw(streams_of[3], (K, R, 2 * PIX), 0.02, 0.125, ((0, 32),))
    part_class = draw_part_class(jax.random.fold_in(streams_of[7], 71), 0)
    part_rot = set_ends(jax.random.randint(streams_of[5], (PARTICLES,), 0, R), jax.random.fold_in(streams_of[5], 1), 0, R - 1).astype(jnp.int32)
    counts = set_ends(jax.random.randint(streams_of[6], (K,), 0, 400), jax.random.fold_in(streams_of[6], 1), 0, 399).astype(jnp.int32)
    return dict(particles=particles, defocus=defocus, inv_noise=inv_noise, references=references, part_class=part_class, part_rot=part_rot, counts=counts)


def frequencies(pixels):
    positions = jnp.arange(pixels, dtype=jnp.int32)
    row_offset = (positions // 64 - pixels // 128).astype(jnp.float32)
    column = (positions % 64).astype(jnp.float32)
    return (row_offset * row_offset + column * column) / 4096.0


def contrast(defocus, inv_noise):
    phase_shift = 12.0 * defocus[:, None] * frequencies(inv_noise.shape[0])[None, :]
    return -0.995 * jnp.sin(phase_shift) - 0.1 * jnp.cos(phase_shift)


def reference(particles, defocus, inv_noise, references, part_class, part_rot, counts):
    contrast_rows = contrast(defocus, inv_noise)
    factor = inv_noise[None, :] * contrast_rows
    weighted = (particles.astype(jnp.float32) * jnp.concatenate([factor, factor], axis=1)).astype(jnp.bfloat16)
    power_weight = (factor * contrast_rows).astype(jnp.bfloat16)
    flat_images = references.reshape(K * R, 2 * PIX).astype(jnp.float32)
    real_part = flat_images[:, :PIX]
    imag_part = flat_images[:, PIX:]
    power = (real_part * real_part + imag_part * imag_part).astype(jnp.bfloat16).astype(jnp.float32)
    log_prior = jnp.log((counts + 1).astype(jnp.float32) / (jnp.sum(counts) + K).astype(jnp.float32))
    prior_rows = jnp.repeat(log_prior, R)
    block_rows = math.gcd(PARTICLES, 512)

    def score_block(operands):
        weight_rows, power_rows = operands
        cross_term = jnp.dot(weight_rows.astype(jnp.float32), flat_images.T, precision=lax.Precision.HIGHEST)
        power_term = jnp.dot(power_rows.astype(jnp.float32), power.T, precision=lax.Precision.HIGHEST)
        return jnp.max(cross_term - 0.5 * power_term + prior_rows[None, :], axis=1)

    best_score = lax.map(score_block, (weighted.reshape(-1, block_rows, 2 * PIX), power_weight.reshape(-1, block_rows, PIX))).reshape(PARTICLES)
    pose_bins = part_class * R + part_rot
    numerator = jax.ops.segment_sum(weighted.astype(jnp.float32), pose_bins, num_segments=K * R)
    denominator = jax.ops.segment_sum(power_weight.astype(jnp.float32), pose_bins, num_segments=K * R)
    images = numerator / (jnp.concatenate([denominator, denominator], axis=1) + 1.0)
    return best_score, images.reshape(K, R, 2 * PIX)
```

```python
import math

import jax
import jax.numpy as jnp
from jax import lax
from jax.experimental import pallas as pl
from jax.sharding import PartitionSpec as P

AMPLITUDE = math.hypot(0.995, 0.1)
PHASE = math.atan2(0.1, 0.995)
ROW_BLOCK = 64


def frequencies(pixels):
    positions = jnp.arange(pixels, dtype=jnp.int32)
    row_offset = (positions // 64 - pixels // 128).astype(jnp.float32)
    column = (positions % 64).astype(jnp.float32)
    return (row_offset * row_offset + column * column) / 4096.0


def weights_kernel(defocus_ref, freq_ref, noise_ref, particles_ref, out_ref):
    pixels = freq_ref.shape[1]
    phase_shift = (12.0 * defocus_ref[...]) * freq_ref[...]
    contrast_rows = -AMPLITUDE * jnp.sin(phase_shift + PHASE)
    factor = noise_ref[...] * contrast_rows
    real_part = particles_ref[:, :pixels].astype(jnp.float32)
    imag_part = particles_ref[:, pixels:].astype(jnp.float32)
    out_ref[:, :pixels] = (real_part * factor).astype(jnp.bfloat16)
    out_ref[:, pixels : 2 * pixels] = (imag_part * factor).astype(jnp.bfloat16)
    out_ref[:, 2 * pixels :] = (factor * contrast_rows).astype(jnp.bfloat16)


def weighted_rows(particles, defocus, inv_noise):
    rows = particles.shape[0]
    pixels = inv_noise.shape[0]
    block = min(ROW_BLOCK, rows)
    return pl.pallas_call(
        weights_kernel,
        grid=(rows // block,),
        in_specs=[
            pl.BlockSpec((block, 1), lambda i: (i, 0)),
            pl.BlockSpec((1, pixels), lambda i: (0, 0)),
            pl.BlockSpec((1, pixels), lambda i: (0, 0)),
            pl.BlockSpec((block, 2 * pixels), lambda i: (i, 0)),
        ],
        out_specs=pl.BlockSpec((block, 3 * pixels), lambda i: (i, 0)),
        out_shape=jax.ShapeDtypeStruct((rows, 3 * pixels), jnp.bfloat16),
    )(defocus[:, None], frequencies(pixels)[None, :], inv_noise[None, :], particles)


def on_device(particles, defocus, inv_noise, references, part_class, part_rot, counts):
    pixels = inv_noise.shape[0]
    owned = references.shape[0]
    rotations = references.shape[1]
    dom_size = lax.axis_size("dom")
    cls_index = lax.axis_index("cls")
    block_classes = dom_size * owned
    block_first = cls_index * block_classes

    images = lax.all_gather(references, "dom", axis=0, tiled=True)
    flat_images = images.reshape(block_classes * rotations, 2 * pixels)
    real_part = flat_images[:, :pixels].astype(jnp.float32)
    imag_part = flat_images[:, pixels:].astype(jnp.float32)
    power = (real_part * real_part + imag_part * imag_part).astype(jnp.bfloat16)
    templates = jnp.concatenate([flat_images, power * jnp.bfloat16(-0.5)], axis=1)

    payload = weighted_rows(particles, defocus, inv_noise)

    class_total = counts.shape[0]
    log_prior = jnp.log(
        (counts + 1).astype(jnp.float32) / (jnp.sum(counts) + class_total).astype(jnp.float32)
    )
    class_prior = lax.dynamic_slice_in_dim(log_prior, block_first, block_classes)
    score = lax.dot_general(
        payload, templates, (((1,), (1,)), ((), ())), preferred_element_type=jnp.float32
    )
    score = score + jnp.repeat(class_prior, rotations)[None, :]
    best_score = lax.pmax(jnp.max(score, axis=1), "cls")

    local_class = part_class - block_first
    in_block = (local_class >= 0) & (local_class < block_classes)
    pose = jnp.where(in_block, local_class * rotations + part_rot, -1)
    poses = jnp.arange(block_classes * rotations, dtype=jnp.int32)
    selector = (poses[:, None] == pose[None, :]).astype(jnp.bfloat16)
    partial = jnp.dot(selector, payload, preferred_element_type=jnp.float32)
    sums = lax.psum_scatter(partial, "dom", scatter_dimension=0, tiled=True)
    numerator = sums[:, : 2 * pixels]
    denominator = sums[:, 2 * pixels :]
    class_images = numerator / (jnp.concatenate([denominator, denominator], axis=1) + 1.0)
    return best_score, class_images.reshape(owned, rotations, 2 * pixels)


def solution(mesh):
    placed = (P("dom", None), P("dom"), P(), P(("cls", "dom"), None, None), P("dom"), P("dom"), P())
    return jax.shard_map(
        on_device,
        mesh=mesh,
        in_specs=placed,
        out_specs=(P("dom"), P(("cls", "dom"), None, None)),
        check_vma=False,
    )
```

```python
import math

import jax
import jax.numpy as jnp
from jax import lax
from jax.experimental import pallas as pl
from jax.sharding import PartitionSpec as P

AMPLITUDE = math.hypot(0.995, 0.1)
PHASE = math.atan2(0.1, 0.995)
ROW_BLOCK = 128


def split_pieces(values, width):
    pieces = []
    rest = values
    for _ in range(3):
        piece = lax.reduce_precision(rest, exponent_bits=8, mantissa_bits=7)
        pieces.append(piece.astype(jnp.bfloat16))
        rest = rest - piece
    joined = jnp.concatenate(pieces, axis=1)
    return jnp.pad(joined, ((0, 0), (0, width - joined.shape[1])))


def contrast_tables(defocus, pixels):
    groups = pixels // 64
    scaled = 12.0 * defocus
    row_offset = (jnp.arange(groups, dtype=jnp.int32) - pixels // 128).astype(jnp.float32)
    row_angle = scaled[:, None] * (row_offset * row_offset / 4096.0)[None, :]
    column = (jnp.arange(128, dtype=jnp.int32) % 64).astype(jnp.float32)
    column_angle = scaled[:, None] * (column * column / 4096.0)[None, :] + PHASE
    width = -(-3 * groups // 128) * 128
    row_sin = split_pieces(-AMPLITUDE * jnp.sin(row_angle), width)
    row_cos = split_pieces(-AMPLITUDE * jnp.cos(row_angle), width)
    slot = jnp.arange(width, dtype=jnp.int32)[:, None]
    group_of = (jnp.arange(pixels, dtype=jnp.int32) // 64)[None, :]
    expand = ((slot < 3 * groups) & (slot % groups == group_of)).astype(jnp.bfloat16)
    return row_sin, row_cos, expand, jnp.cos(column_angle), jnp.sin(column_angle)


def weights_kernel(row_sin_ref, row_cos_ref, expand_ref, col_cos_ref, col_sin_ref, noise_ref, particles_ref, out_ref):
    pixels = noise_ref.shape[1]
    row_sin = jnp.dot(row_sin_ref[...], expand_ref[...], preferred_element_type=jnp.float32)
    row_cos = jnp.dot(row_cos_ref[...], expand_ref[...], preferred_element_type=jnp.float32)
    col_cos = col_cos_ref[...]
    col_sin = col_sin_ref[...]
    for tile in range(pixels // 128):
        lanes = slice(tile * 128, (tile + 1) * 128)
        contrast_rows = row_sin[:, lanes] * col_cos + row_cos[:, lanes] * col_sin
        factor = noise_ref[:, lanes] * contrast_rows
        real_part = particles_ref[:, lanes].astype(jnp.float32)
        imag_part = particles_ref[:, pixels + tile * 128 : pixels + (tile + 1) * 128].astype(jnp.float32)
        out_ref[:, lanes] = (real_part * factor).astype(jnp.bfloat16)
        out_ref[:, pixels + tile * 128 : pixels + (tile + 1) * 128] = (imag_part * factor).astype(jnp.bfloat16)
        out_ref[:, 2 * pixels + tile * 128 : 2 * pixels + (tile + 1) * 128] = (factor * contrast_rows).astype(
            jnp.bfloat16
        )


def weighted_rows(particles, defocus, inv_noise):
    rows = particles.shape[0]
    pixels = inv_noise.shape[0]
    block = min(ROW_BLOCK, rows)
    row_sin, row_cos, expand, col_cos, col_sin = contrast_tables(defocus, pixels)
    width = row_sin.shape[1]
    return pl.pallas_call(
        weights_kernel,
        grid=(rows // block,),
        in_specs=[
            pl.BlockSpec((block, width), lambda i: (i, 0)),
            pl.BlockSpec((block, width), lambda i: (i, 0)),
            pl.BlockSpec((width, pixels), lambda i: (0, 0)),
            pl.BlockSpec((block, 128), lambda i: (i, 0)),
            pl.BlockSpec((block, 128), lambda i: (i, 0)),
            pl.BlockSpec((1, pixels), lambda i: (0, 0)),
            pl.BlockSpec((block, 2 * pixels), lambda i: (i, 0)),
        ],
        out_specs=pl.BlockSpec((block, 3 * pixels), lambda i: (i, 0)),
        out_shape=jax.ShapeDtypeStruct((rows, 3 * pixels), jnp.bfloat16),
    )(row_sin, row_cos, expand, col_cos, col_sin, inv_noise[None, :], particles)


def on_device(particles, defocus, inv_noise, references, part_class, part_rot, counts):
    pixels = inv_noise.shape[0]
    owned = references.shape[0]
    rotations = references.shape[1]
    dom_size = lax.axis_size("dom")
    cls_index = lax.axis_index("cls")
    block_classes = dom_size * owned
    block_first = cls_index * block_classes

    images = lax.all_gather(references, "dom", axis=0, tiled=True)
    flat_images = images.reshape(block_classes * rotations, 2 * pixels)
    real_part = flat_images[:, :pixels].astype(jnp.float32)
    imag_part = flat_images[:, pixels:].astype(jnp.float32)
    power = (real_part * real_part + imag_part * imag_part).astype(jnp.bfloat16)
    templates = jnp.concatenate([flat_images, power * jnp.bfloat16(-0.5)], axis=1)

    payload = weighted_rows(particles, defocus, inv_noise)

    class_total = counts.shape[0]
    log_prior = jnp.log(
        (counts + 1).astype(jnp.float32) / (jnp.sum(counts) + class_total).astype(jnp.float32)
    )
    class_prior = lax.dynamic_slice_in_dim(log_prior, block_first, block_classes)
    score = lax.dot_general(
        payload, templates, (((1,), (1,)), ((), ())), preferred_element_type=jnp.float32
    )
    score = score + jnp.repeat(class_prior, rotations)[None, :]
    best_score = lax.pmax(jnp.max(score, axis=1), "cls")

    local_class = part_class - block_first
    in_block = (local_class >= 0) & (local_class < block_classes)
    pose = jnp.where(in_block, local_class * rotations + part_rot, -1)
    poses = jnp.arange(block_classes * rotations, dtype=jnp.int32)
    selector = (poses[:, None] == pose[None, :]).astype(jnp.bfloat16)
    partial = jnp.dot(selector, payload, preferred_element_type=jnp.float32)
    sums = lax.psum_scatter(partial, "dom", scatter_dimension=0, tiled=True)
    numerator = sums[:, : 2 * pixels]
    denominator = sums[:, 2 * pixels :]
    class_images = numerator / (jnp.concatenate([denominator, denominator], axis=1) + 1.0)
    return best_score, class_images.reshape(owned, rotations, 2 * pixels)


def solution(mesh):
    placed = (P("dom", None), P("dom"), P(), P(("cls", "dom"), None, None), P("dom"), P("dom"), P())
    return jax.shard_map(
        on_device,
        mesh=mesh,
        in_specs=placed,
        out_specs=(P("dom"), P(("cls", "dom"), None, None)),
        check_vma=False,
    )
```

```python
import math

import jax
import jax.numpy as jnp
from jax import lax
from jax.experimental import pallas as pl
from jax.sharding import PartitionSpec as P

AMPLITUDE = math.hypot(0.995, 0.1)
PHASE = math.atan2(0.1, 0.995)
ROW_BLOCK = 128


def split_pieces(values, width):
    pieces = []
    rest = values
    for _ in range(3):
        piece = lax.reduce_precision(rest, exponent_bits=8, mantissa_bits=7)
        pieces.append(piece.astype(jnp.bfloat16))
        rest = rest - piece
    joined = jnp.concatenate(pieces, axis=1)
    return jnp.pad(joined, ((0, 0), (0, width - joined.shape[1])))


def contrast_tables(defocus, pixels):
    groups = pixels // 64
    scaled = 12.0 * defocus
    row_offset = (jnp.arange(groups, dtype=jnp.int32) - pixels // 128).astype(jnp.float32)
    row_angle = scaled[:, None] * (row_offset * row_offset / 4096.0)[None, :]
    column = (jnp.arange(128, dtype=jnp.int32) % 64).astype(jnp.float32)
    column_angle = scaled[:, None] * (column * column / 4096.0)[None, :] + PHASE
    width = -(-3 * groups // 128) * 128
    row_sin = split_pieces(-AMPLITUDE * jnp.sin(row_angle), width)
    row_cos = split_pieces(-AMPLITUDE * jnp.cos(row_angle), width)
    slot = jnp.arange(width, dtype=jnp.int32)[:, None]
    group_of = (jnp.arange(pixels, dtype=jnp.int32) // 64)[None, :]
    expand = ((slot < 3 * groups) & (slot % groups == group_of)).astype(jnp.bfloat16)
    return row_sin, row_cos, expand, jnp.cos(column_angle), jnp.sin(column_angle)


def weights_kernel(row_sin_ref, row_cos_ref, expand_ref, col_cos_ref, col_sin_ref, noise_ref, particles_ref, out_ref):
    pixels = noise_ref.shape[1]
    row_sin = jnp.dot(row_sin_ref[...], expand_ref[...], preferred_element_type=jnp.float32)
    row_cos = jnp.dot(row_cos_ref[...], expand_ref[...], preferred_element_type=jnp.float32)
    col_cos = col_cos_ref[...]
    col_sin = col_sin_ref[...]
    for tile in range(pixels // 128):
        lanes = slice(tile * 128, (tile + 1) * 128)
        contrast_rows = row_sin[:, lanes] * col_cos + row_cos[:, lanes] * col_sin
        factor = noise_ref[:, lanes] * contrast_rows
        real_part = particles_ref[:, lanes].astype(jnp.float32)
        imag_part = particles_ref[:, pixels + tile * 128 : pixels + (tile + 1) * 128].astype(jnp.float32)
        out_ref[:, lanes] = (real_part * factor).astype(jnp.bfloat16)
        out_ref[:, pixels + tile * 128 : pixels + (tile + 1) * 128] = (imag_part * factor).astype(jnp.bfloat16)
        out_ref[:, 2 * pixels + tile * 128 : 2 * pixels + (tile + 1) * 128] = (factor * contrast_rows).astype(
            jnp.bfloat16
        )


def weighted_rows(particles, defocus, inv_noise):
    rows = particles.shape[0]
    pixels = inv_noise.shape[0]
    block = min(ROW_BLOCK, rows)
    row_sin, row_cos, expand, col_cos, col_sin = contrast_tables(defocus, pixels)
    width = row_sin.shape[1]
    return pl.pallas_call(
        weights_kernel,
        grid=(rows // block,),
        in_specs=[
            pl.BlockSpec((block, width), lambda i: (i, 0)),
            pl.BlockSpec((block, width), lambda i: (i, 0)),
            pl.BlockSpec((width, pixels), lambda i: (0, 0)),
            pl.BlockSpec((block, 128), lambda i: (i, 0)),
            pl.BlockSpec((block, 128), lambda i: (i, 0)),
            pl.BlockSpec((1, pixels), lambda i: (0, 0)),
            pl.BlockSpec((block, 2 * pixels), lambda i: (i, 0)),
        ],
        out_specs=pl.BlockSpec((block, 3 * pixels), lambda i: (i, 0)),
        out_shape=jax.ShapeDtypeStruct((rows, 3 * pixels), jnp.bfloat16),
    )(row_sin, row_cos, expand, col_cos, col_sin, inv_noise[None, :], particles)


def on_device(particles, defocus, inv_noise, references, part_class, part_rot, counts):
    pixels = inv_noise.shape[0]
    owned = references.shape[0]
    rotations = references.shape[1]
    dom_size = lax.axis_size("dom")
    cls_index = lax.axis_index("cls")
    block_classes = dom_size * owned
    block_first = cls_index * block_classes

    images = lax.all_gather(references, "dom", axis=0, tiled=True)
    flat_images = images.reshape(block_classes * rotations, 2 * pixels)
    real_part = flat_images[:, :pixels].astype(jnp.float32)
    imag_part = flat_images[:, pixels:].astype(jnp.float32)
    power = (real_part * real_part + imag_part * imag_part).astype(jnp.bfloat16)
    templates = jnp.concatenate([flat_images, power * jnp.bfloat16(-0.5)], axis=1)

    payload = weighted_rows(particles, defocus, inv_noise)

    class_total = counts.shape[0]
    log_prior = jnp.log(
        (counts + 1).astype(jnp.float32) / (jnp.sum(counts) + class_total).astype(jnp.float32)
    )
    class_prior = lax.dynamic_slice_in_dim(log_prior, block_first, block_classes)
    score = lax.dot_general(
        payload, templates, (((1,), (1,)), ((), ())), preferred_element_type=jnp.float32
    )
    score = score + jnp.repeat(class_prior, rotations)[None, :]
    best_score = lax.pmax(jnp.max(score, axis=1), "cls")

    local_class = part_class - block_first
    in_block = (local_class >= 0) & (local_class < block_classes)
    pose = jnp.where(in_block, local_class * rotations + part_rot, -1)
    poses = jnp.arange(block_classes * rotations, dtype=jnp.int32)
    selector = (poses[:, None] == pose[None, :]).astype(jnp.bfloat16)
    partial = jnp.dot(selector, payload, preferred_element_type=jnp.float32)
    sums = lax.psum_scatter(partial.astype(jnp.bfloat16), "dom", scatter_dimension=0, tiled=True)
    sums = sums.astype(jnp.float32)
    numerator = sums[:, : 2 * pixels]
    denominator = sums[:, 2 * pixels :]
    class_images = numerator / (jnp.concatenate([denominator, denominator], axis=1) + 1.0)
    return best_score, class_images.reshape(owned, rotations, 2 * pixels)


def solution(mesh):
    placed = (P("dom", None), P("dom"), P(), P(("cls", "dom"), None, None), P("dom"), P("dom"), P())
    return jax.shard_map(
        on_device,
        mesh=mesh,
        in_specs=placed,
        out_specs=(P("dom"), P(("cls", "dom"), None, None)),
        check_vma=False,
    )
```

```python
import math

import jax
import jax.numpy as jnp
from jax import lax
from jax.experimental import pallas as pl
from jax.sharding import PartitionSpec as P

AMPLITUDE = math.hypot(0.995, 0.1)
PHASE = math.atan2(0.1, 0.995)
ROW_BLOCK = 128


def split_pieces(values, width):
    pieces = []
    rest = values
    for _ in range(3):
        piece = lax.reduce_precision(rest, exponent_bits=8, mantissa_bits=7)
        pieces.append(piece.astype(jnp.bfloat16))
        rest = rest - piece
    joined = jnp.concatenate(pieces, axis=1)
    return jnp.pad(joined, ((0, 0), (0, width - joined.shape[1])))


def contrast_tables(defocus, pixels):
    groups = pixels // 64
    scaled = 12.0 * defocus
    row_offset = (jnp.arange(groups, dtype=jnp.int32) - pixels // 128).astype(jnp.float32)
    row_angle = scaled[:, None] * (row_offset * row_offset / 4096.0)[None, :]
    column = (jnp.arange(128, dtype=jnp.int32) % 64).astype(jnp.float32)
    column_angle = scaled[:, None] * (column * column / 4096.0)[None, :] + PHASE
    width = -(-3 * groups // 128) * 128
    row_sin = split_pieces(-AMPLITUDE * jnp.sin(row_angle), width)
    row_cos = split_pieces(-AMPLITUDE * jnp.cos(row_angle), width)
    slot = jnp.arange(width, dtype=jnp.int32)[:, None]
    group_of = (jnp.arange(pixels, dtype=jnp.int32) // 64)[None, :]
    expand = ((slot < 3 * groups) & (slot % groups == group_of)).astype(jnp.bfloat16)
    return row_sin, row_cos, expand, jnp.cos(column_angle), jnp.sin(column_angle)


def weights_kernel(row_sin_ref, row_cos_ref, expand_ref, col_cos_ref, col_sin_ref, noise_ref, particles_ref, out_ref):
    pixels = noise_ref.shape[1]
    row_sin = jnp.dot(row_sin_ref[...], expand_ref[...], preferred_element_type=jnp.float32)
    row_cos = jnp.dot(row_cos_ref[...], expand_ref[...], preferred_element_type=jnp.float32)
    col_cos = col_cos_ref[...]
    col_sin = col_sin_ref[...]
    for tile in range(pixels // 128):
        lanes = slice(tile * 128, (tile + 1) * 128)
        contrast_rows = row_sin[:, lanes] * col_cos + row_cos[:, lanes] * col_sin
        factor = noise_ref[:, lanes] * contrast_rows
        real_part = particles_ref[:, lanes].astype(jnp.float32)
        imag_part = particles_ref[:, pixels + tile * 128 : pixels + (tile + 1) * 128].astype(jnp.float32)
        out_ref[:, lanes] = (real_part * factor).astype(jnp.bfloat16)
        out_ref[:, pixels + tile * 128 : pixels + (tile + 1) * 128] = (imag_part * factor).astype(jnp.bfloat16)
        out_ref[:, 2 * pixels + tile * 128 : 2 * pixels + (tile + 1) * 128] = (factor * contrast_rows).astype(
            jnp.bfloat16
        )


def weighted_rows(particles, defocus, inv_noise):
    rows = particles.shape[0]
    pixels = inv_noise.shape[0]
    block = min(ROW_BLOCK, rows)
    row_sin, row_cos, expand, col_cos, col_sin = contrast_tables(defocus, pixels)
    width = row_sin.shape[1]
    return pl.pallas_call(
        weights_kernel,
        grid=(rows // block,),
        in_specs=[
            pl.BlockSpec((block, width), lambda i: (i, 0)),
            pl.BlockSpec((block, width), lambda i: (i, 0)),
            pl.BlockSpec((width, pixels), lambda i: (0, 0)),
            pl.BlockSpec((block, 128), lambda i: (i, 0)),
            pl.BlockSpec((block, 128), lambda i: (i, 0)),
            pl.BlockSpec((1, pixels), lambda i: (0, 0)),
            pl.BlockSpec((block, 2 * pixels), lambda i: (i, 0)),
        ],
        out_specs=pl.BlockSpec((block, 3 * pixels), lambda i: (i, 0)),
        out_shape=jax.ShapeDtypeStruct((rows, 3 * pixels), jnp.bfloat16),
    )(row_sin, row_cos, expand, col_cos, col_sin, inv_noise[None, :], particles)


def on_device(particles, defocus, inv_noise, references, part_class, part_rot, counts):
    pixels = inv_noise.shape[0]
    owned = references.shape[0]
    rotations = references.shape[1]
    dom_size = lax.axis_size("dom")
    cls_index = lax.axis_index("cls")
    block_classes = dom_size * owned
    block_first = cls_index * block_classes

    images = lax.all_gather(references, "dom", axis=0, tiled=True)
    flat_images = images.reshape(block_classes * rotations, 2 * pixels)
    real_part = flat_images[:, :pixels].astype(jnp.float32)
    imag_part = flat_images[:, pixels:].astype(jnp.float32)
    power = (real_part * real_part + imag_part * imag_part).astype(jnp.bfloat16)
    templates = jnp.concatenate([flat_images, power * jnp.bfloat16(-0.5)], axis=1)

    payload = weighted_rows(particles, defocus, inv_noise)

    class_total = counts.shape[0]
    log_prior = jnp.log(
        (counts + 1).astype(jnp.float32) / (jnp.sum(counts) + class_total).astype(jnp.float32)
    )
    class_prior = lax.dynamic_slice_in_dim(log_prior, block_first, block_classes)
    score = lax.dot_general(
        payload, templates, (((1,), (1,)), ((), ())), preferred_element_type=jnp.float32
    )
    score = score + jnp.repeat(class_prior, rotations)[None, :]
    best_score = lax.pmax(jnp.max(score, axis=1), "cls")

    dom_index = lax.axis_index("dom")
    chips = dom_size // 2
    chip = dom_index // 2
    core = dom_index % 2
    block_rows = owned * rotations
    local_class = part_class - block_first
    in_block = (local_class >= 0) & (local_class < block_classes)
    owner = local_class // owned
    mine = (owner % 2 == core).astype(jnp.int32)
    offset = (owner // 2 - chip) % chips
    row = ((mine * chips + offset) * owned + local_class % owned) * rotations + part_rot
    row = jnp.where(in_block, row, -1)
    rows = jnp.arange(2 * chips * block_rows, dtype=jnp.int32)
    selector = (rows[:, None] == row[None, :]).astype(jnp.bfloat16)
    partial = jnp.dot(selector, payload, preferred_element_type=jnp.float32)
    partial = partial.reshape(2, chips, block_rows, 3 * pixels)
    partner = [(d, d ^ 1) for d in range(dom_size)]
    chip_sum = partial[1] + lax.ppermute(partial[0], "dom", partner)
    sums = chip_sum[0]
    for shift in range(1, chips):
        pairs = [(d, 2 * ((d // 2 + shift) % chips) + d % 2) for d in range(dom_size)]
        sent = lax.ppermute(chip_sum[shift].astype(jnp.bfloat16), "dom", pairs)
        sums = sums + sent.astype(jnp.float32)
    numerator = sums[:, : 2 * pixels]
    denominator = sums[:, 2 * pixels :]
    class_images = numerator / (jnp.concatenate([denominator, denominator], axis=1) + 1.0)
    return best_score, class_images.reshape(owned, rotations, 2 * pixels)


def solution(mesh):
    placed = (P("dom", None), P("dom"), P(), P(("cls", "dom"), None, None), P("dom"), P("dom"), P())
    return jax.shard_map(
        on_device,
        mesh=mesh,
        in_specs=placed,
        out_specs=(P("dom"), P(("cls", "dom"), None, None)),
        check_vma=False,
    )
```

```python
import math

import jax
import jax.numpy as jnp
from jax import lax
from jax.experimental import pallas as pl
from jax.sharding import Mesh, PartitionSpec as P

AMPLITUDE = math.hypot(0.995, 0.1)
PHASE = math.atan2(0.1, 0.995)
ROW_BLOCK = 128


def split_pieces(values, width):
    pieces = []
    rest = values
    for _ in range(3):
        piece = lax.reduce_precision(rest, exponent_bits=8, mantissa_bits=7)
        pieces.append(piece.astype(jnp.bfloat16))
        rest = rest - piece
    joined = jnp.concatenate(pieces, axis=1)
    return jnp.pad(joined, ((0, 0), (0, width - joined.shape[1])))


def contrast_tables(defocus, pixels):
    groups = pixels // 64
    scaled = 12.0 * defocus
    row_offset = (jnp.arange(groups, dtype=jnp.int32) - pixels // 128).astype(jnp.float32)
    row_angle = scaled[:, None] * (row_offset * row_offset / 4096.0)[None, :]
    column = (jnp.arange(128, dtype=jnp.int32) % 64).astype(jnp.float32)
    column_angle = scaled[:, None] * (column * column / 4096.0)[None, :] + PHASE
    width = -(-3 * groups // 128) * 128
    row_sin = split_pieces(-AMPLITUDE * jnp.sin(row_angle), width)
    row_cos = split_pieces(-AMPLITUDE * jnp.cos(row_angle), width)
    slot = jnp.arange(width, dtype=jnp.int32)[:, None]
    group_of = (jnp.arange(pixels, dtype=jnp.int32) // 64)[None, :]
    expand = ((slot < 3 * groups) & (slot % groups == group_of)).astype(jnp.bfloat16)
    return row_sin, row_cos, expand, jnp.cos(column_angle), jnp.sin(column_angle)


def weights_kernel(row_sin_ref, row_cos_ref, expand_ref, col_cos_ref, col_sin_ref, noise_ref, particles_ref, out_ref):
    pixels = noise_ref.shape[1]
    row_sin = jnp.dot(row_sin_ref[...], expand_ref[...], preferred_element_type=jnp.float32)
    row_cos = jnp.dot(row_cos_ref[...], expand_ref[...], preferred_element_type=jnp.float32)
    col_cos = col_cos_ref[...]
    col_sin = col_sin_ref[...]
    for tile in range(pixels // 128):
        lanes = slice(tile * 128, (tile + 1) * 128)
        contrast_rows = row_sin[:, lanes] * col_cos + row_cos[:, lanes] * col_sin
        factor = noise_ref[:, lanes] * contrast_rows
        real_part = particles_ref[:, lanes].astype(jnp.float32)
        imag_part = particles_ref[:, pixels + tile * 128 : pixels + (tile + 1) * 128].astype(jnp.float32)
        out_ref[:, lanes] = (real_part * factor).astype(jnp.bfloat16)
        out_ref[:, pixels + tile * 128 : pixels + (tile + 1) * 128] = (imag_part * factor).astype(jnp.bfloat16)
        out_ref[:, 2 * pixels + tile * 128 : 2 * pixels + (tile + 1) * 128] = (factor * contrast_rows).astype(
            jnp.bfloat16
        )


def weighted_rows(particles, defocus, inv_noise):
    rows = particles.shape[0]
    pixels = inv_noise.shape[0]
    block = min(ROW_BLOCK, rows)
    row_sin, row_cos, expand, col_cos, col_sin = contrast_tables(defocus, pixels)
    width = row_sin.shape[1]
    return pl.pallas_call(
        weights_kernel,
        grid=(rows // block,),
        in_specs=[
            pl.BlockSpec((block, width), lambda i: (i, 0)),
            pl.BlockSpec((block, width), lambda i: (i, 0)),
            pl.BlockSpec((width, pixels), lambda i: (0, 0)),
            pl.BlockSpec((block, 128), lambda i: (i, 0)),
            pl.BlockSpec((block, 128), lambda i: (i, 0)),
            pl.BlockSpec((1, pixels), lambda i: (0, 0)),
            pl.BlockSpec((block, 2 * pixels), lambda i: (i, 0)),
        ],
        out_specs=pl.BlockSpec((block, 3 * pixels), lambda i: (i, 0)),
        out_shape=jax.ShapeDtypeStruct((rows, 3 * pixels), jnp.bfloat16),
    )(row_sin, row_cos, expand, col_cos, col_sin, inv_noise[None, :], particles)


def on_device(particles, defocus, inv_noise, references, part_class, part_rot, counts):
    pixels = inv_noise.shape[0]
    owned = references.shape[0]
    rotations = references.shape[1]
    dom_size = lax.axis_size(("chip", "core"))
    cls_index = lax.axis_index("cls")
    block_classes = dom_size * owned
    block_first = cls_index * block_classes

    images = lax.all_gather(references, ("chip", "core"), axis=0, tiled=True)
    flat_images = images.reshape(block_classes * rotations, 2 * pixels)
    real_part = flat_images[:, :pixels].astype(jnp.float32)
    imag_part = flat_images[:, pixels:].astype(jnp.float32)
    power = (real_part * real_part + imag_part * imag_part).astype(jnp.bfloat16)
    templates = jnp.concatenate([flat_images, power * jnp.bfloat16(-0.5)], axis=1)

    payload = weighted_rows(particles, defocus, inv_noise)

    class_total = counts.shape[0]
    log_prior = jnp.log(
        (counts + 1).astype(jnp.float32) / (jnp.sum(counts) + class_total).astype(jnp.float32)
    )
    class_prior = lax.dynamic_slice_in_dim(log_prior, block_first, block_classes)
    score = lax.dot_general(
        payload, templates, (((1,), (1,)), ((), ())), preferred_element_type=jnp.float32
    )
    score = score + jnp.repeat(class_prior, rotations)[None, :]
    best_score = lax.pmax(jnp.max(score, axis=1), "cls")

    chips = dom_size // 2
    block_rows = owned * rotations
    local_class = part_class - block_first
    in_block = (local_class >= 0) & (local_class < block_classes)
    owner = local_class // owned
    row = (((owner % 2) * chips + owner // 2) * owned + local_class % owned) * rotations + part_rot
    row = jnp.where(in_block, row, -1)
    rows = jnp.arange(dom_size * block_rows, dtype=jnp.int32)
    selector = (rows[:, None] == row[None, :]).astype(jnp.bfloat16)
    partial = jnp.dot(selector, payload, preferred_element_type=jnp.float32)
    chip_sums = lax.psum_scatter(partial, "core", scatter_dimension=0, tiled=True)
    sums = lax.psum_scatter(chip_sums.astype(jnp.bfloat16), "chip", scatter_dimension=0, tiled=True)
    sums = sums.astype(jnp.float32)
    numerator = sums[:, : 2 * pixels]
    denominator = sums[:, 2 * pixels :]
    class_images = numerator / (jnp.concatenate([denominator, denominator], axis=1) + 1.0)
    return best_score, class_images.reshape(owned, rotations, 2 * pixels)


def solution(mesh):
    dom_size, cls_size = mesh.devices.shape
    split = Mesh(mesh.devices.reshape(dom_size // 2, 2, cls_size), ("chip", "core", "cls"))
    dom = ("chip", "core")
    placed = (P(dom, None), P(dom), P(), P(("cls",) + dom, None, None), P(dom), P(dom), P())
    return jax.shard_map(
        on_device,
        mesh=split,
        in_specs=placed,
        out_specs=(P(dom), P(("cls",) + dom, None, None)),
        check_vma=False,
    )
```

```python
import math

import jax
import jax.numpy as jnp
from jax import lax
from jax.experimental import pallas as pl
from jax.sharding import PartitionSpec as P

AMPLITUDE = math.hypot(0.995, 0.1)
PHASE = math.atan2(0.1, 0.995)
ROW_BLOCK = 128


def split_pieces(values, width):
    pieces = []
    rest = values
    for _ in range(3):
        piece = lax.reduce_precision(rest, exponent_bits=8, mantissa_bits=7)
        pieces.append(piece.astype(jnp.bfloat16))
        rest = rest - piece
    joined = jnp.concatenate(pieces, axis=1)
    return jnp.pad(joined, ((0, 0), (0, width - joined.shape[1])))


def contrast_tables(defocus, pixels):
    groups = pixels // 64
    scaled = 12.0 * defocus
    row_offset = (jnp.arange(groups, dtype=jnp.int32) - pixels // 128).astype(jnp.float32)
    row_angle = scaled[:, None] * (row_offset * row_offset / 4096.0)[None, :]
    column = (jnp.arange(128, dtype=jnp.int32) % 64).astype(jnp.float32)
    column_angle = scaled[:, None] * (column * column / 4096.0)[None, :] + PHASE
    width = -(-3 * groups // 128) * 128
    row_sin = split_pieces(-AMPLITUDE * jnp.sin(row_angle), width)
    row_cos = split_pieces(-AMPLITUDE * jnp.cos(row_angle), width)
    slot = jnp.arange(width, dtype=jnp.int32)[:, None]
    group_of = (jnp.arange(pixels, dtype=jnp.int32) // 64)[None, :]
    expand = ((slot < 3 * groups) & (slot % groups == group_of)).astype(jnp.bfloat16)
    return row_sin, row_cos, expand, jnp.cos(column_angle), jnp.sin(column_angle)


def contrast_tile(row_sin, row_cos, col_cos, col_sin, tile):
    lanes = slice(tile * 128, (tile + 1) * 128)
    return row_sin[:, lanes] * col_cos + row_cos[:, lanes] * col_sin


def weights_kernel(row_sin_ref, row_cos_ref, expand_ref, col_cos_ref, col_sin_ref, noise_ref, particles_ref, out_ref, power_ref):
    pixels = noise_ref.shape[1]
    row_sin = jnp.dot(row_sin_ref[...], expand_ref[...], preferred_element_type=jnp.float32)
    row_cos = jnp.dot(row_cos_ref[...], expand_ref[...], preferred_element_type=jnp.float32)
    col_cos = col_cos_ref[...]
    col_sin = col_sin_ref[...]
    for tile in range(pixels // 128):
        lanes = slice(tile * 128, (tile + 1) * 128)
        imag = slice(pixels + tile * 128, pixels + (tile + 1) * 128)
        contrast_rows = contrast_tile(row_sin, row_cos, col_cos, col_sin, tile)
        factor = noise_ref[:, lanes] * contrast_rows
        out_ref[:, lanes] = (particles_ref[:, lanes].astype(jnp.float32) * factor).astype(jnp.bfloat16)
        out_ref[:, imag] = (particles_ref[:, imag].astype(jnp.float32) * factor).astype(jnp.bfloat16)
        power_ref[:, lanes] = (factor * contrast_rows).astype(jnp.bfloat16)


def power_kernel(row_sin_ref, row_cos_ref, expand_ref, col_cos_ref, col_sin_ref, noise_ref, power_ref):
    pixels = noise_ref.shape[1]
    row_sin = jnp.dot(row_sin_ref[...], expand_ref[...], preferred_element_type=jnp.float32)
    row_cos = jnp.dot(row_cos_ref[...], expand_ref[...], preferred_element_type=jnp.float32)
    col_cos = col_cos_ref[...]
    col_sin = col_sin_ref[...]
    for tile in range(pixels // 128):
        lanes = slice(tile * 128, (tile + 1) * 128)
        contrast_rows = contrast_tile(row_sin, row_cos, col_cos, col_sin, tile)
        factor = noise_ref[:, lanes] * contrast_rows
        power_ref[:, lanes] = (factor * contrast_rows).astype(jnp.bfloat16)


def table_specs(block, width, pixels):
    return [
        pl.BlockSpec((block, width), lambda i: (i, 0)),
        pl.BlockSpec((block, width), lambda i: (i, 0)),
        pl.BlockSpec((width, pixels), lambda i: (0, 0)),
        pl.BlockSpec((block, 128), lambda i: (i, 0)),
        pl.BlockSpec((block, 128), lambda i: (i, 0)),
        pl.BlockSpec((1, pixels), lambda i: (0, 0)),
    ]


def weighted_rows(particles, defocus, inv_noise):
    rows = particles.shape[0]
    pixels = inv_noise.shape[0]
    block = min(ROW_BLOCK, rows)
    tables = contrast_tables(defocus, pixels)
    width = tables[0].shape[1]
    return pl.pallas_call(
        weights_kernel,
        grid=(rows // block,),
        in_specs=table_specs(block, width, pixels) + [pl.BlockSpec((block, 2 * pixels), lambda i: (i, 0))],
        out_specs=[
            pl.BlockSpec((block, 2 * pixels), lambda i: (i, 0)),
            pl.BlockSpec((block, pixels), lambda i: (i, 0)),
        ],
        out_shape=[
            jax.ShapeDtypeStruct((rows, 2 * pixels), jnp.bfloat16),
            jax.ShapeDtypeStruct((rows, pixels), jnp.bfloat16),
        ],
    )(*tables, inv_noise[None, :], particles)


def power_rows(defocus, inv_noise):
    rows = defocus.shape[0]
    pixels = inv_noise.shape[0]
    block = min(ROW_BLOCK, rows)
    tables = contrast_tables(defocus, pixels)
    width = tables[0].shape[1]
    return pl.pallas_call(
        power_kernel,
        grid=(rows // block,),
        in_specs=table_specs(block, width, pixels),
        out_specs=pl.BlockSpec((block, pixels), lambda i: (i, 0)),
        out_shape=jax.ShapeDtypeStruct((rows, pixels), jnp.bfloat16),
    )(*tables, inv_noise[None, :])


def on_device(particles, defocus, inv_noise, references, part_class, part_rot, counts):
    local_rows = particles.shape[0]
    pixels = inv_noise.shape[0]
    owned = references.shape[0]
    rotations = references.shape[1]
    dom_size = lax.axis_size("dom")
    cls_size = lax.axis_size("cls")
    cls_index = lax.axis_index("cls")
    block_classes = dom_size * owned
    block_first = cls_index * block_classes
    own_first = (block_first + lax.axis_index("dom") * owned) * rotations

    images = lax.all_gather(references, "dom", axis=0, tiled=True)
    flat_images = images.reshape(block_classes * rotations, 2 * pixels)
    real_part = flat_images[:, :pixels].astype(jnp.float32)
    imag_part = flat_images[:, pixels:].astype(jnp.float32)
    power = (real_part * real_part + imag_part * imag_part).astype(jnp.bfloat16)

    weighted, power_weight = weighted_rows(particles, defocus, inv_noise)

    local_class = part_class - block_first
    in_block = (local_class >= 0) & (local_class < block_classes)
    pose = jnp.where(in_block, local_class * rotations + part_rot, -1)
    poses = jnp.arange(block_classes * rotations, dtype=jnp.int32)
    selector = (poses[:, None] == pose[None, :]).astype(jnp.bfloat16)
    partial = jnp.dot(selector, weighted, preferred_element_type=jnp.float32)
    numerator = lax.psum_scatter(partial, "dom", scatter_dimension=0, tiled=True)

    class_total = counts.shape[0]
    log_prior = jnp.log(
        (counts + 1).astype(jnp.float32) / (jnp.sum(counts) + class_total).astype(jnp.float32)
    )
    class_prior = lax.dynamic_slice_in_dim(log_prior, block_first, block_classes)
    score = lax.dot_general(
        weighted, flat_images, (((1,), (1,)), ((), ())), preferred_element_type=jnp.float32
    ) + lax.dot_general(
        power_weight, power * jnp.bfloat16(-0.5), (((1,), (1,)), ((), ())), preferred_element_type=jnp.float32
    )
    score = score + jnp.repeat(class_prior, rotations)[None, :]
    best_score = lax.pmax(jnp.max(score, axis=1), "cls")

    capacity = max(2, 3 * local_rows // (dom_size * cls_size))
    slots = dom_size * capacity
    every_defocus = lax.all_gather(defocus, "dom", axis=0, tiled=True)
    every_pose = lax.all_gather(part_class * rotations + part_rot, "dom", axis=0, tiled=True)
    own_pose = every_pose - own_first
    owned_here = (own_pose >= 0) & (own_pose < owned * rotations)
    running = jnp.cumsum(owned_here.astype(jnp.int32))
    slot_ids = jnp.arange(slots, dtype=jnp.int32)
    source = jnp.minimum(jnp.searchsorted(running, slot_ids + 1), every_pose.shape[0] - 1)
    filled = slot_ids < running[-1]
    slot_defocus = jnp.where(filled, jnp.take(every_defocus, source), 1.0)
    slot_pose = jnp.where(filled, jnp.take(own_pose, source), -1)
    slot_power = power_rows(slot_defocus, inv_noise)
    own_poses = jnp.arange(owned * rotations, dtype=jnp.int32)
    gather_own = (own_poses[:, None] == slot_pose[None, :]).astype(jnp.bfloat16)
    denominator = jnp.dot(gather_own, slot_power, preferred_element_type=jnp.float32)

    class_images = numerator / (jnp.concatenate([denominator, denominator], axis=1) + 1.0)
    return best_score, class_images.reshape(owned, rotations, 2 * pixels)


def solution(mesh):
    placed = (P("dom", None), P("dom"), P(), P(("cls", "dom"), None, None), P("dom"), P("dom"), P())
    return jax.shard_map(
        on_device,
        mesh=mesh,
        in_specs=placed,
        out_specs=(P("dom"), P(("cls", "dom"), None, None)),
        check_vma=False,
    )
```

```python
import math

import jax
import jax.numpy as jnp
from jax import lax
from jax.experimental import pallas as pl
from jax.sharding import PartitionSpec as P

AMPLITUDE = math.hypot(0.995, 0.1)
PHASE = math.atan2(0.1, 0.995)
ROW_BLOCK = 128


def split_pieces(values, width):
    pieces = []
    rest = values
    for _ in range(3):
        piece = lax.reduce_precision(rest, exponent_bits=8, mantissa_bits=7)
        pieces.append(piece.astype(jnp.bfloat16))
        rest = rest - piece
    joined = jnp.concatenate(pieces, axis=1)
    return jnp.pad(joined, ((0, 0), (0, width - joined.shape[1])))


def contrast_tables(defocus, pixels):
    groups = pixels // 64
    scaled = 12.0 * defocus
    row_offset = (jnp.arange(groups, dtype=jnp.int32) - pixels // 128).astype(jnp.float32)
    row_angle = scaled[:, None] * (row_offset * row_offset / 4096.0)[None, :]
    column = (jnp.arange(128, dtype=jnp.int32) % 64).astype(jnp.float32)
    column_angle = scaled[:, None] * (column * column / 4096.0)[None, :] + PHASE
    width = -(-3 * groups // 128) * 128
    row_sin = split_pieces(-AMPLITUDE * jnp.sin(row_angle), width)
    row_cos = split_pieces(-AMPLITUDE * jnp.cos(row_angle), width)
    slot = jnp.arange(width, dtype=jnp.int32)[:, None]
    group_of = (jnp.arange(pixels, dtype=jnp.int32) // 64)[None, :]
    expand = ((slot < 3 * groups) & (slot % groups == group_of)).astype(jnp.bfloat16)
    return row_sin, row_cos, expand, jnp.cos(column_angle), jnp.sin(column_angle)


def contrast_tile(row_sin, row_cos, col_cos, col_sin, tile):
    lanes = slice(tile * 128, (tile + 1) * 128)
    return row_sin[:, lanes] * col_cos + row_cos[:, lanes] * col_sin


def weights_kernel(row_sin_ref, row_cos_ref, expand_ref, col_cos_ref, col_sin_ref, noise_ref, particles_ref, out_ref, power_ref):
    pixels = noise_ref.shape[1]
    row_sin = jnp.dot(row_sin_ref[...], expand_ref[...], preferred_element_type=jnp.float32)
    row_cos = jnp.dot(row_cos_ref[...], expand_ref[...], preferred_element_type=jnp.float32)
    col_cos = col_cos_ref[...]
    col_sin = col_sin_ref[...]
    for tile in range(pixels // 128):
        lanes = slice(tile * 128, (tile + 1) * 128)
        imag = slice(pixels + tile * 128, pixels + (tile + 1) * 128)
        contrast_rows = contrast_tile(row_sin, row_cos, col_cos, col_sin, tile)
        factor = noise_ref[:, lanes] * contrast_rows
        out_ref[:, lanes] = (particles_ref[:, lanes].astype(jnp.float32) * factor).astype(jnp.bfloat16)
        out_ref[:, imag] = (particles_ref[:, imag].astype(jnp.float32) * factor).astype(jnp.bfloat16)
        power_ref[:, lanes] = (factor * contrast_rows).astype(jnp.bfloat16)


def power_kernel(row_sin_ref, row_cos_ref, expand_ref, col_cos_ref, col_sin_ref, noise_ref, power_ref):
    pixels = noise_ref.shape[1]
    row_sin = jnp.dot(row_sin_ref[...], expand_ref[...], preferred_element_type=jnp.float32)
    row_cos = jnp.dot(row_cos_ref[...], expand_ref[...], preferred_element_type=jnp.float32)
    col_cos = col_cos_ref[...]
    col_sin = col_sin_ref[...]
    for tile in range(pixels // 128):
        lanes = slice(tile * 128, (tile + 1) * 128)
        contrast_rows = contrast_tile(row_sin, row_cos, col_cos, col_sin, tile)
        factor = noise_ref[:, lanes] * contrast_rows
        power_ref[:, lanes] = (factor * contrast_rows).astype(jnp.bfloat16)


def table_specs(block, width, pixels):
    return [
        pl.BlockSpec((block, width), lambda i: (i, 0)),
        pl.BlockSpec((block, width), lambda i: (i, 0)),
        pl.BlockSpec((width, pixels), lambda i: (0, 0)),
        pl.BlockSpec((block, 128), lambda i: (i, 0)),
        pl.BlockSpec((block, 128), lambda i: (i, 0)),
        pl.BlockSpec((1, pixels), lambda i: (0, 0)),
    ]


def weighted_rows(particles, defocus, inv_noise):
    rows = particles.shape[0]
    pixels = inv_noise.shape[0]
    block = min(ROW_BLOCK, rows)
    tables = contrast_tables(defocus, pixels)
    width = tables[0].shape[1]
    return pl.pallas_call(
        weights_kernel,
        grid=(rows // block,),
        in_specs=table_specs(block, width, pixels) + [pl.BlockSpec((block, 2 * pixels), lambda i: (i, 0))],
        out_specs=[
            pl.BlockSpec((block, 2 * pixels), lambda i: (i, 0)),
            pl.BlockSpec((block, pixels), lambda i: (i, 0)),
        ],
        out_shape=[
            jax.ShapeDtypeStruct((rows, 2 * pixels), jnp.bfloat16),
            jax.ShapeDtypeStruct((rows, pixels), jnp.bfloat16),
        ],
    )(*tables, inv_noise[None, :], particles)


def power_rows(defocus, inv_noise):
    rows = defocus.shape[0]
    pixels = inv_noise.shape[0]
    block = min(ROW_BLOCK, rows)
    tables = contrast_tables(defocus, pixels)
    width = tables[0].shape[1]
    return pl.pallas_call(
        power_kernel,
        grid=(rows // block,),
        in_specs=table_specs(block, width, pixels),
        out_specs=pl.BlockSpec((block, pixels), lambda i: (i, 0)),
        out_shape=jax.ShapeDtypeStruct((rows, pixels), jnp.bfloat16),
    )(*tables, inv_noise[None, :])


def on_device(particles, defocus, inv_noise, references, part_class, part_rot, counts):
    local_rows = particles.shape[0]
    pixels = inv_noise.shape[0]
    owned = references.shape[0]
    rotations = references.shape[1]
    dom_size = lax.axis_size("dom")
    cls_size = lax.axis_size("cls")
    cls_index = lax.axis_index("cls")
    block_classes = dom_size * owned
    block_first = cls_index * block_classes

    local_class = part_class - block_first
    facts = split_pieces(defocus[None, :], 3 * local_rows).reshape(3, local_rows)
    block_class = jnp.clip(local_class, -1, block_classes).astype(jnp.bfloat16)
    facts = jnp.concatenate([facts, block_class[None, :], part_rot.astype(jnp.bfloat16)[None, :]], axis=0)
    extra_rows = -(-facts.size // (2 * pixels))
    facts = jnp.pad(facts.reshape(-1), (0, extra_rows * 2 * pixels - facts.size))
    ref_rows = owned * rotations
    sending = jnp.concatenate(
        [references.reshape(ref_rows, 2 * pixels), facts.reshape(extra_rows, 2 * pixels)], axis=0
    )
    gathered = lax.all_gather(sending, "dom", axis=0, tiled=False)
    flat_images = gathered[:, :ref_rows].reshape(block_classes * rotations, 2 * pixels)
    every_fact = gathered[:, ref_rows:].reshape(dom_size, -1)[:, : 5 * local_rows]
    every_fact = every_fact.reshape(dom_size, 5, local_rows).transpose(1, 0, 2).reshape(5, dom_size * local_rows)
    real_part = flat_images[:, :pixels].astype(jnp.float32)
    imag_part = flat_images[:, pixels:].astype(jnp.float32)
    power = (real_part * real_part + imag_part * imag_part).astype(jnp.bfloat16)

    weighted, power_weight = weighted_rows(particles, defocus, inv_noise)

    in_block = (local_class >= 0) & (local_class < block_classes)
    pose = jnp.where(in_block, local_class * rotations + part_rot, -1)
    poses = jnp.arange(block_classes * rotations, dtype=jnp.int32)
    selector = (poses[:, None] == pose[None, :]).astype(jnp.bfloat16)
    partial = jnp.dot(selector, weighted, preferred_element_type=jnp.float32)
    numerator = lax.psum_scatter(partial, "dom", scatter_dimension=0, tiled=True)

    class_total = counts.shape[0]
    log_prior = jnp.log(
        (counts + 1).astype(jnp.float32) / (jnp.sum(counts) + class_total).astype(jnp.float32)
    )
    class_prior = lax.dynamic_slice_in_dim(log_prior, block_first, block_classes)
    score = lax.dot_general(
        weighted, flat_images, (((1,), (1,)), ((), ())), preferred_element_type=jnp.float32
    ) + lax.dot_general(
        power_weight, power * jnp.bfloat16(-0.5), (((1,), (1,)), ((), ())), preferred_element_type=jnp.float32
    )
    score = score + jnp.repeat(class_prior, rotations)[None, :]
    best_score = lax.pmax(jnp.max(score, axis=1), "cls")

    capacity = max(2, 3 * local_rows // (dom_size * cls_size))
    slots = dom_size * capacity
    fact_class = every_fact[3].astype(jnp.float32).astype(jnp.int32) - lax.axis_index("dom") * owned
    owned_here = (fact_class >= 0) & (fact_class < owned)
    running = jnp.cumsum(owned_here.astype(jnp.int32))
    slot_of = jnp.where(owned_here, running - 1, -1)
    slot_ids = jnp.arange(slots, dtype=jnp.int32)
    picker = (slot_ids[:, None] == slot_of[None, :]).astype(jnp.bfloat16)
    picked = lax.dot_general(
        every_fact, picker, (((1,), (1,)), ((), ())), preferred_element_type=jnp.float32
    )
    filled = slot_ids < running[-1]
    slot_defocus = jnp.where(filled, (picked[0] + picked[1]) + picked[2], 1.0)
    slot_pose = picked[3].astype(jnp.int32) - lax.axis_index("dom") * owned
    slot_pose = jnp.where(filled, slot_pose * rotations + picked[4].astype(jnp.int32), -1)
    slot_power = power_rows(slot_defocus, inv_noise)
    own_poses = jnp.arange(owned * rotations, dtype=jnp.int32)
    gather_own = (own_poses[:, None] == slot_pose[None, :]).astype(jnp.bfloat16)
    denominator = jnp.dot(gather_own, slot_power, preferred_element_type=jnp.float32)

    class_images = numerator / (jnp.concatenate([denominator, denominator], axis=1) + 1.0)
    return best_score, class_images.reshape(owned, rotations, 2 * pixels)


def solution(mesh):
    placed = (P("dom", None), P("dom"), P(), P(("cls", "dom"), None, None), P("dom"), P("dom"), P())
    return jax.shard_map(
        on_device,
        mesh=mesh,
        in_specs=placed,
        out_specs=(P("dom"), P(("cls", "dom"), None, None)),
        check_vma=False,
    )
```

```python
import math

import jax
import jax.numpy as jnp
from jax import lax
from jax.experimental import pallas as pl
from jax.sharding import PartitionSpec as P

AMPLITUDE = math.hypot(0.995, 0.1)
PHASE = math.atan2(0.1, 0.995)
ROW_BLOCK = 128


def split_pieces(values, width):
    pieces = []
    rest = values
    for _ in range(3):
        piece = lax.reduce_precision(rest, exponent_bits=8, mantissa_bits=7)
        pieces.append(piece.astype(jnp.bfloat16))
        rest = rest - piece
    joined = jnp.concatenate(pieces, axis=1)
    return jnp.pad(joined, ((0, 0), (0, width - joined.shape[1])))


def contrast_tables(defocus, pixels):
    groups = pixels // 64
    scaled = 12.0 * defocus
    row_offset = (jnp.arange(groups, dtype=jnp.int32) - pixels // 128).astype(jnp.float32)
    row_angle = scaled[:, None] * (row_offset * row_offset / 4096.0)[None, :]
    column = (jnp.arange(128, dtype=jnp.int32) % 64).astype(jnp.float32)
    column_angle = scaled[:, None] * (column * column / 4096.0)[None, :] + PHASE
    width = -(-3 * groups // 128) * 128
    row_sin = split_pieces(-AMPLITUDE * jnp.sin(row_angle), width)
    row_cos = split_pieces(-AMPLITUDE * jnp.cos(row_angle), width)
    slot = jnp.arange(width, dtype=jnp.int32)[:, None]
    group_of = (jnp.arange(pixels, dtype=jnp.int32) // 64)[None, :]
    expand = ((slot < 3 * groups) & (slot % groups == group_of)).astype(jnp.bfloat16)
    return row_sin, row_cos, expand, jnp.cos(column_angle), jnp.sin(column_angle)


def contrast_tile(row_sin, row_cos, col_cos, col_sin, tile):
    lanes = slice(tile * 128, (tile + 1) * 128)
    return row_sin[:, lanes] * col_cos + row_cos[:, lanes] * col_sin


def weights_kernel(
    row_sin_ref, row_cos_ref, expand_ref, col_cos_ref, col_sin_ref, noise_ref, particles_ref, selector_ref,
    out_ref, power_ref, sums_ref,
):
    pixels = noise_ref.shape[1]
    row_sin = jnp.dot(row_sin_ref[...], expand_ref[...], preferred_element_type=jnp.float32)
    row_cos = jnp.dot(row_cos_ref[...], expand_ref[...], preferred_element_type=jnp.float32)
    col_cos = col_cos_ref[...]
    col_sin = col_sin_ref[...]
    for tile in range(pixels // 128):
        lanes = slice(tile * 128, (tile + 1) * 128)
        imag = slice(pixels + tile * 128, pixels + (tile + 1) * 128)
        contrast_rows = contrast_tile(row_sin, row_cos, col_cos, col_sin, tile)
        factor = noise_ref[:, lanes] * contrast_rows
        out_ref[:, lanes] = (particles_ref[:, lanes].astype(jnp.float32) * factor).astype(jnp.bfloat16)
        out_ref[:, imag] = (particles_ref[:, imag].astype(jnp.float32) * factor).astype(jnp.bfloat16)
        power_ref[:, lanes] = (factor * contrast_rows).astype(jnp.bfloat16)

    @pl.when(pl.program_id(0) == 0)
    def _():
        sums_ref[...] = jnp.zeros_like(sums_ref)

    sums_ref[...] += jnp.dot(selector_ref[...], out_ref[...], preferred_element_type=jnp.float32)


def power_kernel(row_sin_ref, row_cos_ref, expand_ref, col_cos_ref, col_sin_ref, noise_ref, power_ref):
    pixels = noise_ref.shape[1]
    row_sin = jnp.dot(row_sin_ref[...], expand_ref[...], preferred_element_type=jnp.float32)
    row_cos = jnp.dot(row_cos_ref[...], expand_ref[...], preferred_element_type=jnp.float32)
    col_cos = col_cos_ref[...]
    col_sin = col_sin_ref[...]
    for tile in range(pixels // 128):
        lanes = slice(tile * 128, (tile + 1) * 128)
        contrast_rows = contrast_tile(row_sin, row_cos, col_cos, col_sin, tile)
        factor = noise_ref[:, lanes] * contrast_rows
        power_ref[:, lanes] = (factor * contrast_rows).astype(jnp.bfloat16)


def table_specs(block, width, pixels):
    return [
        pl.BlockSpec((block, width), lambda i: (i, 0)),
        pl.BlockSpec((block, width), lambda i: (i, 0)),
        pl.BlockSpec((width, pixels), lambda i: (0, 0)),
        pl.BlockSpec((block, 128), lambda i: (i, 0)),
        pl.BlockSpec((block, 128), lambda i: (i, 0)),
        pl.BlockSpec((1, pixels), lambda i: (0, 0)),
    ]


def weighted_rows(particles, defocus, inv_noise, selector):
    rows = particles.shape[0]
    poses = selector.shape[0]
    pixels = inv_noise.shape[0]
    block = min(ROW_BLOCK, rows)
    tables = contrast_tables(defocus, pixels)
    width = tables[0].shape[1]
    return pl.pallas_call(
        weights_kernel,
        grid=(rows // block,),
        in_specs=table_specs(block, width, pixels)
        + [pl.BlockSpec((block, 2 * pixels), lambda i: (i, 0)), pl.BlockSpec((poses, block), lambda i: (0, i))],
        out_specs=[
            pl.BlockSpec((block, 2 * pixels), lambda i: (i, 0)),
            pl.BlockSpec((block, pixels), lambda i: (i, 0)),
            pl.BlockSpec((poses, 2 * pixels), lambda i: (0, 0)),
        ],
        out_shape=[
            jax.ShapeDtypeStruct((rows, 2 * pixels), jnp.bfloat16),
            jax.ShapeDtypeStruct((rows, pixels), jnp.bfloat16),
            jax.ShapeDtypeStruct((poses, 2 * pixels), jnp.float32),
        ],
    )(*tables, inv_noise[None, :], particles, selector)


def power_rows(defocus, inv_noise):
    rows = defocus.shape[0]
    pixels = inv_noise.shape[0]
    block = min(ROW_BLOCK, rows)
    tables = contrast_tables(defocus, pixels)
    width = tables[0].shape[1]
    return pl.pallas_call(
        power_kernel,
        grid=(rows // block,),
        in_specs=table_specs(block, width, pixels),
        out_specs=pl.BlockSpec((block, pixels), lambda i: (i, 0)),
        out_shape=jax.ShapeDtypeStruct((rows, pixels), jnp.bfloat16),
    )(*tables, inv_noise[None, :])


def on_device(particles, defocus, inv_noise, references, part_class, part_rot, counts):
    local_rows = particles.shape[0]
    pixels = inv_noise.shape[0]
    owned = references.shape[0]
    rotations = references.shape[1]
    dom_size = lax.axis_size("dom")
    cls_size = lax.axis_size("cls")
    cls_index = lax.axis_index("cls")
    block_classes = dom_size * owned
    block_first = cls_index * block_classes

    local_class = part_class - block_first
    facts = split_pieces(defocus[None, :], 3 * local_rows).reshape(3, local_rows)
    block_class = jnp.clip(local_class, -1, block_classes).astype(jnp.bfloat16)
    facts = jnp.concatenate([facts, block_class[None, :], part_rot.astype(jnp.bfloat16)[None, :]], axis=0)
    extra_rows = -(-facts.size // (2 * pixels))
    facts = jnp.pad(facts.reshape(-1), (0, extra_rows * 2 * pixels - facts.size))
    ref_rows = owned * rotations
    sending = jnp.concatenate(
        [references.reshape(ref_rows, 2 * pixels), facts.reshape(extra_rows, 2 * pixels)], axis=0
    )
    gathered = lax.all_gather(sending, "dom", axis=0, tiled=False)
    flat_images = gathered[:, :ref_rows].reshape(block_classes * rotations, 2 * pixels)
    every_fact = gathered[:, ref_rows:].reshape(dom_size, -1)[:, : 5 * local_rows]
    every_fact = every_fact.reshape(dom_size, 5, local_rows).transpose(1, 0, 2).reshape(5, dom_size * local_rows)
    real_part = flat_images[:, :pixels].astype(jnp.float32)
    imag_part = flat_images[:, pixels:].astype(jnp.float32)
    power = (real_part * real_part + imag_part * imag_part).astype(jnp.bfloat16)

    in_block = (local_class >= 0) & (local_class < block_classes)
    pose = jnp.where(in_block, local_class * rotations + part_rot, -1)
    poses = jnp.arange(block_classes * rotations, dtype=jnp.int32)
    selector = (poses[:, None] == pose[None, :]).astype(jnp.bfloat16)
    weighted, power_weight, partial = weighted_rows(particles, defocus, inv_noise, selector)
    numerator = lax.psum_scatter(partial, "dom", scatter_dimension=0, tiled=True)

    class_total = counts.shape[0]
    log_prior = jnp.log(
        (counts + 1).astype(jnp.float32) / (jnp.sum(counts) + class_total).astype(jnp.float32)
    )
    class_prior = lax.dynamic_slice_in_dim(log_prior, block_first, block_classes)
    score = lax.dot_general(
        weighted, flat_images, (((1,), (1,)), ((), ())), preferred_element_type=jnp.float32
    ) + lax.dot_general(
        power_weight, power * jnp.bfloat16(-0.5), (((1,), (1,)), ((), ())), preferred_element_type=jnp.float32
    )
    score = score + jnp.repeat(class_prior, rotations)[None, :]
    best_score = lax.pmax(jnp.max(score, axis=1), "cls")

    capacity = max(2, 3 * local_rows // (dom_size * cls_size))
    slots = dom_size * capacity
    fact_class = every_fact[3].astype(jnp.float32).astype(jnp.int32) - lax.axis_index("dom") * owned
    owned_here = (fact_class >= 0) & (fact_class < owned)
    running = jnp.cumsum(owned_here.astype(jnp.int32))
    slot_of = jnp.where(owned_here, running - 1, -1)
    slot_ids = jnp.arange(slots, dtype=jnp.int32)
    picker = (slot_ids[:, None] == slot_of[None, :]).astype(jnp.bfloat16)
    picked = lax.dot_general(
        every_fact, picker, (((1,), (1,)), ((), ())), preferred_element_type=jnp.float32
    )
    filled = slot_ids < running[-1]
    slot_defocus = jnp.where(filled, (picked[0] + picked[1]) + picked[2], 1.0)
    slot_pose = picked[3].astype(jnp.int32) - lax.axis_index("dom") * owned
    slot_pose = jnp.where(filled, slot_pose * rotations + picked[4].astype(jnp.int32), -1)
    slot_power = power_rows(slot_defocus, inv_noise)
    own_poses = jnp.arange(owned * rotations, dtype=jnp.int32)
    gather_own = (own_poses[:, None] == slot_pose[None, :]).astype(jnp.bfloat16)
    denominator = jnp.dot(gather_own, slot_power, preferred_element_type=jnp.float32)

    class_images = numerator / (jnp.concatenate([denominator, denominator], axis=1) + 1.0)
    return best_score, class_images.reshape(owned, rotations, 2 * pixels)


def solution(mesh):
    placed = (P("dom", None), P("dom"), P(), P(("cls", "dom"), None, None), P("dom"), P("dom"), P())
    return jax.shard_map(
        on_device,
        mesh=mesh,
        in_specs=placed,
        out_specs=(P("dom"), P(("cls", "dom"), None, None)),
        check_vma=False,
    )
```

```python
import math

import jax
import jax.numpy as jnp
from jax import lax
from jax.experimental import pallas as pl
from jax.sharding import PartitionSpec as P

AMPLITUDE = math.hypot(0.995, 0.1)
PHASE = math.atan2(0.1, 0.995)
ROW_BLOCK = 128


def split_pieces(values, width):
    pieces = []
    rest = values
    for _ in range(3):
        piece = lax.reduce_precision(rest, exponent_bits=8, mantissa_bits=7)
        pieces.append(piece.astype(jnp.bfloat16))
        rest = rest - piece
    joined = jnp.concatenate(pieces, axis=1)
    return jnp.pad(joined, ((0, 0), (0, width - joined.shape[1])))


def contrast_tables(defocus, pixels):
    groups = pixels // 64
    scaled = 12.0 * defocus
    row_offset = (jnp.arange(groups, dtype=jnp.int32) - pixels // 128).astype(jnp.float32)
    row_angle = scaled[:, None] * (row_offset * row_offset / 4096.0)[None, :]
    column = (jnp.arange(128, dtype=jnp.int32) % 64).astype(jnp.float32)
    column_angle = scaled[:, None] * (column * column / 4096.0)[None, :] + PHASE
    width = -(-3 * groups // 128) * 128
    row_sin = split_pieces(-AMPLITUDE * jnp.sin(row_angle), width)
    row_cos = split_pieces(-AMPLITUDE * jnp.cos(row_angle), width)
    slot = jnp.arange(width, dtype=jnp.int32)[:, None]
    group_of = (jnp.arange(pixels, dtype=jnp.int32) // 64)[None, :]
    expand = ((slot < 3 * groups) & (slot % groups == group_of)).astype(jnp.bfloat16)
    return row_sin, row_cos, expand, jnp.cos(column_angle), jnp.sin(column_angle)


def contrast_tile(row_sin, row_cos, col_cos, col_sin, tile):
    lanes = slice(tile * 128, (tile + 1) * 128)
    return row_sin[:, lanes] * col_cos + row_cos[:, lanes] * col_sin


def weights_kernel(
    row_sin_ref, row_cos_ref, expand_ref, col_cos_ref, col_sin_ref, noise_ref, particles_ref, selector_ref,
    out_ref, power_ref, sums_ref,
):
    pixels = noise_ref.shape[1]
    row_sin = jnp.dot(row_sin_ref[...], expand_ref[...], preferred_element_type=jnp.float32)
    row_cos = jnp.dot(row_cos_ref[...], expand_ref[...], preferred_element_type=jnp.float32)
    col_cos = col_cos_ref[...]
    col_sin = col_sin_ref[...]
    for tile in range(pixels // 128):
        lanes = slice(tile * 128, (tile + 1) * 128)
        imag = slice(pixels + tile * 128, pixels + (tile + 1) * 128)
        contrast_rows = contrast_tile(row_sin, row_cos, col_cos, col_sin, tile)
        factor = noise_ref[:, lanes] * contrast_rows
        out_ref[:, lanes] = (particles_ref[:, lanes].astype(jnp.float32) * factor).astype(jnp.bfloat16)
        out_ref[:, imag] = (particles_ref[:, imag].astype(jnp.float32) * factor).astype(jnp.bfloat16)
        power_ref[:, lanes] = (factor * contrast_rows).astype(jnp.bfloat16)

    @pl.when(pl.program_id(0) == 0)
    def _():
        sums_ref[...] = jnp.zeros_like(sums_ref)

    sums_ref[...] += jnp.dot(selector_ref[...], out_ref[...], preferred_element_type=jnp.float32)


def power_kernel(row_sin_ref, row_cos_ref, expand_ref, col_cos_ref, col_sin_ref, noise_ref, power_ref):
    pixels = noise_ref.shape[1]
    row_sin = jnp.dot(row_sin_ref[...], expand_ref[...], preferred_element_type=jnp.float32)
    row_cos = jnp.dot(row_cos_ref[...], expand_ref[...], preferred_element_type=jnp.float32)
    col_cos = col_cos_ref[...]
    col_sin = col_sin_ref[...]
    for tile in range(pixels // 128):
        lanes = slice(tile * 128, (tile + 1) * 128)
        contrast_rows = contrast_tile(row_sin, row_cos, col_cos, col_sin, tile)
        factor = noise_ref[:, lanes] * contrast_rows
        power_ref[:, lanes] = (factor * contrast_rows).astype(jnp.bfloat16)


def table_specs(block, width, pixels):
    return [
        pl.BlockSpec((block, width), lambda i: (i, 0)),
        pl.BlockSpec((block, width), lambda i: (i, 0)),
        pl.BlockSpec((width, pixels), lambda i: (0, 0)),
        pl.BlockSpec((block, 128), lambda i: (i, 0)),
        pl.BlockSpec((block, 128), lambda i: (i, 0)),
        pl.BlockSpec((1, pixels), lambda i: (0, 0)),
    ]


def weighted_rows(particles, defocus, inv_noise, selector):
    rows = particles.shape[0]
    poses = selector.shape[0]
    pixels = inv_noise.shape[0]
    block = min(ROW_BLOCK, rows)
    tables = contrast_tables(defocus, pixels)
    width = tables[0].shape[1]
    return pl.pallas_call(
        weights_kernel,
        grid=(rows // block,),
        in_specs=table_specs(block, width, pixels)
        + [pl.BlockSpec((block, 2 * pixels), lambda i: (i, 0)), pl.BlockSpec((poses, block), lambda i: (0, i))],
        out_specs=[
            pl.BlockSpec((block, 2 * pixels), lambda i: (i, 0)),
            pl.BlockSpec((block, pixels), lambda i: (i, 0)),
            pl.BlockSpec((poses, 2 * pixels), lambda i: (0, 0)),
        ],
        out_shape=[
            jax.ShapeDtypeStruct((rows, 2 * pixels), jnp.bfloat16),
            jax.ShapeDtypeStruct((rows, pixels), jnp.bfloat16),
            jax.ShapeDtypeStruct((poses, 2 * pixels), jnp.float32),
        ],
    )(*tables, inv_noise[None, :], particles, selector)


def power_rows(defocus, inv_noise):
    rows = defocus.shape[0]
    pixels = inv_noise.shape[0]
    block = min(ROW_BLOCK, rows)
    tables = contrast_tables(defocus, pixels)
    width = tables[0].shape[1]
    return pl.pallas_call(
        power_kernel,
        grid=(rows // block,),
        in_specs=table_specs(block, width, pixels),
        out_specs=pl.BlockSpec((block, pixels), lambda i: (i, 0)),
        out_shape=jax.ShapeDtypeStruct((rows, pixels), jnp.bfloat16),
    )(*tables, inv_noise[None, :])


def on_device(particles, defocus, inv_noise, references, part_class, part_rot, counts):
    local_rows = particles.shape[0]
    pixels = inv_noise.shape[0]
    owned = references.shape[0]
    rotations = references.shape[1]
    dom_size = lax.axis_size("dom")
    cls_size = lax.axis_size("cls")
    cls_index = lax.axis_index("cls")
    block_classes = dom_size * owned
    block_first = cls_index * block_classes

    local_class = part_class - block_first
    facts = split_pieces(defocus[None, :], 3 * local_rows).reshape(3, local_rows)
    block_class = jnp.clip(local_class, -1, block_classes).astype(jnp.bfloat16)
    facts = jnp.concatenate([facts, block_class[None, :], part_rot.astype(jnp.bfloat16)[None, :]], axis=0)
    ref_rows = owned * rotations
    extra_lanes = -(-facts.size // (ref_rows * 128)) * 128
    facts = jnp.pad(facts.reshape(-1), (0, extra_lanes * ref_rows - facts.size))
    sending = jnp.concatenate(
        [references.reshape(ref_rows, 2 * pixels), facts.reshape(ref_rows, extra_lanes)], axis=1
    )
    gathered = lax.all_gather(sending, "dom", axis=0, tiled=False)
    flat_images = gathered[:, :, : 2 * pixels].reshape(block_classes * rotations, 2 * pixels)
    every_fact = gathered[:, :, 2 * pixels :].reshape(dom_size, -1)[:, : 5 * local_rows]
    every_fact = every_fact.reshape(dom_size, 5, local_rows).transpose(1, 0, 2).reshape(5, dom_size * local_rows)
    real_part = flat_images[:, :pixels].astype(jnp.float32)
    imag_part = flat_images[:, pixels:].astype(jnp.float32)
    power = (real_part * real_part + imag_part * imag_part).astype(jnp.bfloat16)

    in_block = (local_class >= 0) & (local_class < block_classes)
    pose = jnp.where(in_block, local_class * rotations + part_rot, -1)
    poses = jnp.arange(block_classes * rotations, dtype=jnp.int32)
    selector = (poses[:, None] == pose[None, :]).astype(jnp.bfloat16)
    weighted, power_weight, partial = weighted_rows(particles, defocus, inv_noise, selector)
    numerator = lax.psum_scatter(partial, "dom", scatter_dimension=0, tiled=True)

    class_total = counts.shape[0]
    log_prior = jnp.log(
        (counts + 1).astype(jnp.float32) / (jnp.sum(counts) + class_total).astype(jnp.float32)
    )
    class_prior = lax.dynamic_slice_in_dim(log_prior, block_first, block_classes)
    score = lax.dot_general(
        weighted, flat_images, (((1,), (1,)), ((), ())), preferred_element_type=jnp.float32
    ) + lax.dot_general(
        power_weight, power * jnp.bfloat16(-0.5), (((1,), (1,)), ((), ())), preferred_element_type=jnp.float32
    )
    score = score + jnp.repeat(class_prior, rotations)[None, :]
    best_score = lax.pmax(jnp.max(score, axis=1), "cls")

    capacity = max(2, 3 * local_rows // (dom_size * cls_size))
    slots = dom_size * capacity
    fact_class = every_fact[3].astype(jnp.float32).astype(jnp.int32) - lax.axis_index("dom") * owned
    owned_here = (fact_class >= 0) & (fact_class < owned)
    running = jnp.cumsum(owned_here.astype(jnp.int32))
    slot_of = jnp.where(owned_here, running - 1, -1)
    slot_ids = jnp.arange(slots, dtype=jnp.int32)
    picker = (slot_ids[:, None] == slot_of[None, :]).astype(jnp.bfloat16)
    picked = lax.dot_general(
        every_fact, picker, (((1,), (1,)), ((), ())), preferred_element_type=jnp.float32
    )
    filled = slot_ids < running[-1]
    slot_defocus = jnp.where(filled, (picked[0] + picked[1]) + picked[2], 1.0)
    slot_pose = picked[3].astype(jnp.int32) - lax.axis_index("dom") * owned
    slot_pose = jnp.where(filled, slot_pose * rotations + picked[4].astype(jnp.int32), -1)
    slot_power = power_rows(slot_defocus, inv_noise)
    own_poses = jnp.arange(owned * rotations, dtype=jnp.int32)
    gather_own = (own_poses[:, None] == slot_pose[None, :]).astype(jnp.bfloat16)
    denominator = jnp.dot(gather_own, slot_power, preferred_element_type=jnp.float32)

    class_images = numerator / (jnp.concatenate([denominator, denominator], axis=1) + 1.0)
    return best_score, class_images.reshape(owned, rotations, 2 * pixels)


def solution(mesh):
    placed = (P("dom", None), P("dom"), P(), P(("cls", "dom"), None, None), P("dom"), P("dom"), P())
    return jax.shard_map(
        on_device,
        mesh=mesh,
        in_specs=placed,
        out_specs=(P("dom"), P(("cls", "dom"), None, None)),
        check_vma=False,
    )
```

```python
import math

import jax
import jax.numpy as jnp
from jax import lax
from jax.experimental import pallas as pl
from jax.sharding import Mesh, PartitionSpec as P

AMPLITUDE = math.hypot(0.995, 0.1)
PHASE = math.atan2(0.1, 0.995)
ROW_BLOCK = 128


def split_pieces(values, width):
    pieces = []
    rest = values
    for _ in range(3):
        piece = lax.reduce_precision(rest, exponent_bits=8, mantissa_bits=7)
        pieces.append(piece.astype(jnp.bfloat16))
        rest = rest - piece
    joined = jnp.concatenate(pieces, axis=1)
    return jnp.pad(joined, ((0, 0), (0, width - joined.shape[1])))


def contrast_tables(defocus, pixels):
    groups = pixels // 64
    scaled = 12.0 * defocus
    row_offset = (jnp.arange(groups, dtype=jnp.int32) - pixels // 128).astype(jnp.float32)
    row_angle = scaled[:, None] * (row_offset * row_offset / 4096.0)[None, :]
    column = (jnp.arange(128, dtype=jnp.int32) % 64).astype(jnp.float32)
    column_angle = scaled[:, None] * (column * column / 4096.0)[None, :] + PHASE
    width = -(-3 * groups // 128) * 128
    row_sin = split_pieces(-AMPLITUDE * jnp.sin(row_angle), width)
    row_cos = split_pieces(-AMPLITUDE * jnp.cos(row_angle), width)
    slot = jnp.arange(width, dtype=jnp.int32)[:, None]
    group_of = (jnp.arange(pixels, dtype=jnp.int32) // 64)[None, :]
    expand = ((slot < 3 * groups) & (slot % groups == group_of)).astype(jnp.bfloat16)
    return row_sin, row_cos, expand, jnp.cos(column_angle), jnp.sin(column_angle)


def contrast_tile(row_sin, row_cos, col_cos, col_sin, tile):
    lanes = slice(tile * 128, (tile + 1) * 128)
    return row_sin[:, lanes] * col_cos + row_cos[:, lanes] * col_sin


def weights_kernel(
    row_sin_ref, row_cos_ref, expand_ref, col_cos_ref, col_sin_ref, noise_ref, particles_ref, selector_ref,
    out_ref, power_ref, sums_ref,
):
    pixels = noise_ref.shape[1]
    row_sin = jnp.dot(row_sin_ref[...], expand_ref[...], preferred_element_type=jnp.float32)
    row_cos = jnp.dot(row_cos_ref[...], expand_ref[...], preferred_element_type=jnp.float32)
    col_cos = col_cos_ref[...]
    col_sin = col_sin_ref[...]
    for tile in range(pixels // 128):
        lanes = slice(tile * 128, (tile + 1) * 128)
        imag = slice(pixels + tile * 128, pixels + (tile + 1) * 128)
        contrast_rows = contrast_tile(row_sin, row_cos, col_cos, col_sin, tile)
        factor = noise_ref[:, lanes] * contrast_rows
        out_ref[:, lanes] = (particles_ref[:, lanes].astype(jnp.float32) * factor).astype(jnp.bfloat16)
        out_ref[:, imag] = (particles_ref[:, imag].astype(jnp.float32) * factor).astype(jnp.bfloat16)
        power_ref[:, lanes] = (factor * contrast_rows).astype(jnp.bfloat16)

    @pl.when(pl.program_id(0) == 0)
    def _():
        sums_ref[...] = jnp.zeros_like(sums_ref)

    sums_ref[...] += jnp.dot(selector_ref[...], out_ref[...], preferred_element_type=jnp.float32)


def power_kernel(row_sin_ref, row_cos_ref, expand_ref, col_cos_ref, col_sin_ref, noise_ref, power_ref):
    pixels = noise_ref.shape[1]
    row_sin = jnp.dot(row_sin_ref[...], expand_ref[...], preferred_element_type=jnp.float32)
    row_cos = jnp.dot(row_cos_ref[...], expand_ref[...], preferred_element_type=jnp.float32)
    col_cos = col_cos_ref[...]
    col_sin = col_sin_ref[...]
    for tile in range(pixels // 128):
        lanes = slice(tile * 128, (tile + 1) * 128)
        contrast_rows = contrast_tile(row_sin, row_cos, col_cos, col_sin, tile)
        factor = noise_ref[:, lanes] * contrast_rows
        power_ref[:, lanes] = (factor * contrast_rows).astype(jnp.bfloat16)


def table_specs(block, width, pixels):
    return [
        pl.BlockSpec((block, width), lambda i: (i, 0)),
        pl.BlockSpec((block, width), lambda i: (i, 0)),
        pl.BlockSpec((width, pixels), lambda i: (0, 0)),
        pl.BlockSpec((block, 128), lambda i: (i, 0)),
        pl.BlockSpec((block, 128), lambda i: (i, 0)),
        pl.BlockSpec((1, pixels), lambda i: (0, 0)),
    ]


def weighted_rows(particles, defocus, inv_noise, selector):
    rows = particles.shape[0]
    poses = selector.shape[0]
    pixels = inv_noise.shape[0]
    block = min(ROW_BLOCK, rows)
    tables = contrast_tables(defocus, pixels)
    width = tables[0].shape[1]
    return pl.pallas_call(
        weights_kernel,
        grid=(rows // block,),
        in_specs=table_specs(block, width, pixels)
        + [pl.BlockSpec((block, 2 * pixels), lambda i: (i, 0)), pl.BlockSpec((poses, block), lambda i: (0, i))],
        out_specs=[
            pl.BlockSpec((block, 2 * pixels), lambda i: (i, 0)),
            pl.BlockSpec((block, pixels), lambda i: (i, 0)),
            pl.BlockSpec((poses, 2 * pixels), lambda i: (0, 0)),
        ],
        out_shape=[
            jax.ShapeDtypeStruct((rows, 2 * pixels), jnp.bfloat16),
            jax.ShapeDtypeStruct((rows, pixels), jnp.bfloat16),
            jax.ShapeDtypeStruct((poses, 2 * pixels), jnp.float32),
        ],
    )(*tables, inv_noise[None, :], particles, selector)


def power_rows(defocus, inv_noise):
    rows = defocus.shape[0]
    pixels = inv_noise.shape[0]
    block = min(ROW_BLOCK, rows)
    tables = contrast_tables(defocus, pixels)
    width = tables[0].shape[1]
    return pl.pallas_call(
        power_kernel,
        grid=(rows // block,),
        in_specs=table_specs(block, width, pixels),
        out_specs=pl.BlockSpec((block, pixels), lambda i: (i, 0)),
        out_shape=jax.ShapeDtypeStruct((rows, pixels), jnp.bfloat16),
    )(*tables, inv_noise[None, :])


def on_device(particles, defocus, inv_noise, references, part_class, part_rot, counts):
    local_rows = particles.shape[0]
    pixels = inv_noise.shape[0]
    owned = references.shape[0]
    rotations = references.shape[1]
    chips = lax.axis_size("chip")
    dom_size = 2 * chips
    cls_size = lax.axis_size("cls")
    cls_index = lax.axis_index("cls")
    chip = lax.axis_index("chip")
    core = lax.axis_index("core")
    dom_index = 2 * chip + core
    block_classes = dom_size * owned
    block_first = cls_index * block_classes
    swap = [(0, 1), (1, 0)]

    local_class = part_class - block_first
    facts = split_pieces(defocus[None, :], 3 * local_rows).reshape(3, local_rows)
    block_class = jnp.clip(local_class, -1, block_classes).astype(jnp.bfloat16)
    facts = jnp.concatenate([facts, block_class[None, :], part_rot.astype(jnp.bfloat16)[None, :]], axis=0)
    ref_rows = owned * rotations
    extra_lanes = -(-facts.size // (ref_rows * 128)) * 128
    facts = jnp.pad(facts.reshape(-1), (0, extra_lanes * ref_rows - facts.size))
    sending = jnp.concatenate(
        [references.reshape(ref_rows, 2 * pixels), facts.reshape(ref_rows, extra_lanes)], axis=1
    )
    fetched = lax.all_gather(sending, "chip", axis=0, tiled=False)
    gathered = jnp.stack([fetched, lax.ppermute(fetched, "core", swap)])
    flat_images = gathered[:, :, :, : 2 * pixels].reshape(block_classes * rotations, 2 * pixels)
    every_fact = gathered[:, :, :, 2 * pixels :].reshape(dom_size, -1)[:, : 5 * local_rows]
    row_ids = jnp.arange(block_classes * rotations, dtype=jnp.int32) // rotations
    row_core = jnp.where(row_ids // (chips * owned) == 0, core, 1 - core)
    row_block = 2 * ((row_ids // owned) % chips) + row_core
    row_class = block_first + row_block * owned + row_ids % owned
    every_fact = every_fact.reshape(dom_size, 5, local_rows).transpose(1, 0, 2).reshape(5, dom_size * local_rows)
    real_part = flat_images[:, :pixels].astype(jnp.float32)
    imag_part = flat_images[:, pixels:].astype(jnp.float32)
    power = (real_part * real_part + imag_part * imag_part).astype(jnp.bfloat16)

    in_block = (local_class >= 0) & (local_class < block_classes)
    owner = local_class // owned
    mine = (owner % 2 == core).astype(jnp.int32)
    pose = ((mine * chips + owner // 2) * owned + local_class % owned) * rotations + part_rot
    pose = jnp.where(in_block, pose, -1)
    poses = jnp.arange(block_classes * rotations, dtype=jnp.int32)
    selector = (poses[:, None] == pose[None, :]).astype(jnp.bfloat16)
    weighted, power_weight, partial = weighted_rows(particles, defocus, inv_noise, selector)
    partial = partial.reshape(2, chips * owned * rotations, 2 * pixels)
    chip_sums = partial[1] + lax.ppermute(partial[0], "core", swap)
    numerator = lax.psum_scatter(chip_sums, "chip", scatter_dimension=0, tiled=True)

    class_total = counts.shape[0]
    log_prior = jnp.log(
        (counts + 1).astype(jnp.float32) / (jnp.sum(counts) + class_total).astype(jnp.float32)
    )
    score = lax.dot_general(
        weighted, flat_images, (((1,), (1,)), ((), ())), preferred_element_type=jnp.float32
    ) + lax.dot_general(
        power_weight, power * jnp.bfloat16(-0.5), (((1,), (1,)), ((), ())), preferred_element_type=jnp.float32
    )
    score = score + jnp.take(log_prior, row_class)[None, :]
    best_score = lax.pmax(jnp.max(score, axis=1), "cls")

    capacity = max(2, 3 * local_rows // (dom_size * cls_size))
    slots = dom_size * capacity
    fact_class = every_fact[3].astype(jnp.float32).astype(jnp.int32) - dom_index * owned
    owned_here = (fact_class >= 0) & (fact_class < owned)
    running = jnp.cumsum(owned_here.astype(jnp.int32))
    slot_of = jnp.where(owned_here, running - 1, -1)
    slot_ids = jnp.arange(slots, dtype=jnp.int32)
    picker = (slot_ids[:, None] == slot_of[None, :]).astype(jnp.bfloat16)
    picked = lax.dot_general(
        every_fact, picker, (((1,), (1,)), ((), ())), preferred_element_type=jnp.float32
    )
    filled = slot_ids < running[-1]
    slot_defocus = jnp.where(filled, (picked[0] + picked[1]) + picked[2], 1.0)
    slot_pose = picked[3].astype(jnp.int32) - dom_index * owned
    slot_pose = jnp.where(filled, slot_pose * rotations + picked[4].astype(jnp.int32), -1)
    slot_power = power_rows(slot_defocus, inv_noise)
    own_poses = jnp.arange(owned * rotations, dtype=jnp.int32)
    gather_own = (own_poses[:, None] == slot_pose[None, :]).astype(jnp.bfloat16)
    denominator = jnp.dot(gather_own, slot_power, preferred_element_type=jnp.float32)

    class_images = numerator / (jnp.concatenate([denominator, denominator], axis=1) + 1.0)
    return best_score, class_images.reshape(owned, rotations, 2 * pixels)


def solution(mesh):
    dom_size, cls_size = mesh.devices.shape
    split = Mesh(mesh.devices.reshape(dom_size // 2, 2, cls_size), ("chip", "core", "cls"))
    dom = ("chip", "core")
    placed = (P(dom, None), P(dom), P(), P(("cls",) + dom, None, None), P(dom), P(dom), P())
    return jax.shard_map(
        on_device,
        mesh=split,
        in_specs=placed,
        out_specs=(P(dom), P(("cls",) + dom, None, None)),
        check_vma=False,
    )
```

```python
import math

import jax
import jax.numpy as jnp
from jax import lax
from jax.experimental import pallas as pl
from jax.sharding import Mesh, PartitionSpec as P

AMPLITUDE = math.hypot(0.995, 0.1)
PHASE = math.atan2(0.1, 0.995)
ROW_BLOCK = 128


def split_pieces(values, width):
    pieces = []
    rest = values
    for _ in range(3):
        piece = lax.reduce_precision(rest, exponent_bits=8, mantissa_bits=7)
        pieces.append(piece.astype(jnp.bfloat16))
        rest = rest - piece
    joined = jnp.concatenate(pieces, axis=1)
    return jnp.pad(joined, ((0, 0), (0, width - joined.shape[1])))


def contrast_tables(defocus, pixels):
    groups = pixels // 64
    scaled = 12.0 * defocus
    row_offset = (jnp.arange(groups, dtype=jnp.int32) - pixels // 128).astype(jnp.float32)
    row_angle = scaled[:, None] * (row_offset * row_offset / 4096.0)[None, :]
    column = (jnp.arange(128, dtype=jnp.int32) % 64).astype(jnp.float32)
    column_angle = scaled[:, None] * (column * column / 4096.0)[None, :] + PHASE
    width = -(-3 * groups // 128) * 128
    row_sin = split_pieces(-AMPLITUDE * jnp.sin(row_angle), width)
    row_cos = split_pieces(-AMPLITUDE * jnp.cos(row_angle), width)
    slot = jnp.arange(width, dtype=jnp.int32)[:, None]
    group_of = (jnp.arange(pixels, dtype=jnp.int32) // 64)[None, :]
    expand = ((slot < 3 * groups) & (slot % groups == group_of)).astype(jnp.bfloat16)
    return row_sin, row_cos, expand, jnp.cos(column_angle), jnp.sin(column_angle)


def contrast_tile(row_sin, row_cos, col_cos, col_sin, tile):
    lanes = slice(tile * 128, (tile + 1) * 128)
    return row_sin[:, lanes] * col_cos + row_cos[:, lanes] * col_sin


def weights_kernel(
    row_sin_ref, row_cos_ref, expand_ref, col_cos_ref, col_sin_ref, noise_ref, particles_ref, selector_ref,
    out_ref, power_ref, sums_ref,
):
    pixels = noise_ref.shape[1]
    row_sin = jnp.dot(row_sin_ref[...], expand_ref[...], preferred_element_type=jnp.float32)
    row_cos = jnp.dot(row_cos_ref[...], expand_ref[...], preferred_element_type=jnp.float32)
    col_cos = col_cos_ref[...]
    col_sin = col_sin_ref[...]
    for tile in range(pixels // 128):
        lanes = slice(tile * 128, (tile + 1) * 128)
        imag = slice(pixels + tile * 128, pixels + (tile + 1) * 128)
        contrast_rows = contrast_tile(row_sin, row_cos, col_cos, col_sin, tile)
        factor = noise_ref[:, lanes] * contrast_rows
        out_ref[:, lanes] = (particles_ref[:, lanes].astype(jnp.float32) * factor).astype(jnp.bfloat16)
        out_ref[:, imag] = (particles_ref[:, imag].astype(jnp.float32) * factor).astype(jnp.bfloat16)
        power_ref[:, lanes] = (factor * contrast_rows).astype(jnp.bfloat16)

    @pl.when(pl.program_id(0) == 0)
    def _():
        sums_ref[...] = jnp.zeros_like(sums_ref)

    sums_ref[...] += jnp.dot(selector_ref[...], out_ref[...], preferred_element_type=jnp.float32)


def power_kernel(row_sin_ref, row_cos_ref, expand_ref, col_cos_ref, col_sin_ref, noise_ref, power_ref):
    pixels = noise_ref.shape[1]
    row_sin = jnp.dot(row_sin_ref[...], expand_ref[...], preferred_element_type=jnp.float32)
    row_cos = jnp.dot(row_cos_ref[...], expand_ref[...], preferred_element_type=jnp.float32)
    col_cos = col_cos_ref[...]
    col_sin = col_sin_ref[...]
    for tile in range(pixels // 128):
        lanes = slice(tile * 128, (tile + 1) * 128)
        contrast_rows = contrast_tile(row_sin, row_cos, col_cos, col_sin, tile)
        factor = noise_ref[:, lanes] * contrast_rows
        power_ref[:, lanes] = (factor * contrast_rows).astype(jnp.bfloat16)


def table_specs(block, width, pixels):
    return [
        pl.BlockSpec((block, width), lambda i: (i, 0)),
        pl.BlockSpec((block, width), lambda i: (i, 0)),
        pl.BlockSpec((width, pixels), lambda i: (0, 0)),
        pl.BlockSpec((block, 128), lambda i: (i, 0)),
        pl.BlockSpec((block, 128), lambda i: (i, 0)),
        pl.BlockSpec((1, pixels), lambda i: (0, 0)),
    ]


def weighted_rows(particles, defocus, inv_noise, selector):
    rows = particles.shape[0]
    poses = selector.shape[0]
    pixels = inv_noise.shape[0]
    block = min(ROW_BLOCK, rows)
    tables = contrast_tables(defocus, pixels)
    width = tables[0].shape[1]
    return pl.pallas_call(
        weights_kernel,
        grid=(rows // block,),
        in_specs=table_specs(block, width, pixels)
        + [pl.BlockSpec((block, 2 * pixels), lambda i: (i, 0)), pl.BlockSpec((poses, block), lambda i: (0, i))],
        out_specs=[
            pl.BlockSpec((block, 2 * pixels), lambda i: (i, 0)),
            pl.BlockSpec((block, pixels), lambda i: (i, 0)),
            pl.BlockSpec((poses, 2 * pixels), lambda i: (0, 0)),
        ],
        out_shape=[
            jax.ShapeDtypeStruct((rows, 2 * pixels), jnp.bfloat16),
            jax.ShapeDtypeStruct((rows, pixels), jnp.bfloat16),
            jax.ShapeDtypeStruct((poses, 2 * pixels), jnp.float32),
        ],
    )(*tables, inv_noise[None, :], particles, selector)


def power_rows(defocus, inv_noise):
    rows = defocus.shape[0]
    pixels = inv_noise.shape[0]
    block = min(ROW_BLOCK, rows)
    tables = contrast_tables(defocus, pixels)
    width = tables[0].shape[1]
    return pl.pallas_call(
        power_kernel,
        grid=(rows // block,),
        in_specs=table_specs(block, width, pixels),
        out_specs=pl.BlockSpec((block, pixels), lambda i: (i, 0)),
        out_shape=jax.ShapeDtypeStruct((rows, pixels), jnp.bfloat16),
    )(*tables, inv_noise[None, :])


def on_device(particles, defocus, inv_noise, references, part_class, part_rot, counts):
    local_rows = particles.shape[0]
    pixels = inv_noise.shape[0]
    owned = references.shape[0]
    rotations = references.shape[1]
    chips = lax.axis_size("chip")
    dom_size = 2 * chips
    cls_size = lax.axis_size("cls")
    cls_index = lax.axis_index("cls")
    chip = lax.axis_index("chip")
    core = lax.axis_index("core")
    dom_index = 2 * chip + core
    block_classes = dom_size * owned
    block_first = cls_index * block_classes
    swap = [(0, 1), (1, 0)]

    local_class = part_class - block_first
    facts = split_pieces(defocus[None, :], 3 * local_rows).reshape(3, local_rows)
    block_class = jnp.clip(local_class, -1, block_classes).astype(jnp.bfloat16)
    facts = jnp.concatenate([facts, block_class[None, :], part_rot.astype(jnp.bfloat16)[None, :]], axis=0)
    ref_rows = owned * rotations
    extra_lanes = -(-facts.size // (ref_rows * 128)) * 128
    facts = jnp.pad(facts.reshape(-1), (0, extra_lanes * ref_rows - facts.size))
    sending = jnp.concatenate(
        [references.reshape(ref_rows, 2 * pixels), facts.reshape(ref_rows, extra_lanes)], axis=1
    )
    gathered = lax.all_gather(sending, ("chip", "core"), axis=0, tiled=False)
    flat_images = gathered[:, :, : 2 * pixels].reshape(block_classes * rotations, 2 * pixels)
    every_fact = gathered[:, :, 2 * pixels :].reshape(dom_size, -1)[:, : 5 * local_rows]
    row_class = block_first + jnp.arange(block_classes * rotations, dtype=jnp.int32) // rotations
    every_fact = every_fact.reshape(dom_size, 5, local_rows).transpose(1, 0, 2).reshape(5, dom_size * local_rows)
    real_part = flat_images[:, :pixels].astype(jnp.float32)
    imag_part = flat_images[:, pixels:].astype(jnp.float32)
    power = (real_part * real_part + imag_part * imag_part).astype(jnp.bfloat16)

    in_block = (local_class >= 0) & (local_class < block_classes)
    owner = local_class // owned
    mine = (owner % 2 == core).astype(jnp.int32)
    pose = ((mine * chips + owner // 2) * owned + local_class % owned) * rotations + part_rot
    pose = jnp.where(in_block, pose, -1)
    poses = jnp.arange(block_classes * rotations, dtype=jnp.int32)
    selector = (poses[:, None] == pose[None, :]).astype(jnp.bfloat16)
    weighted, power_weight, partial = weighted_rows(particles, defocus, inv_noise, selector)
    partial = partial.reshape(2, chips * owned * rotations, 2 * pixels)
    chip_sums = partial[1] + lax.ppermute(partial[0], "core", swap)
    numerator = lax.psum_scatter(chip_sums, "chip", scatter_dimension=0, tiled=True)

    class_total = counts.shape[0]
    log_prior = jnp.log(
        (counts + 1).astype(jnp.float32) / (jnp.sum(counts) + class_total).astype(jnp.float32)
    )
    score = lax.dot_general(
        weighted, flat_images, (((1,), (1,)), ((), ())), preferred_element_type=jnp.float32
    ) + lax.dot_general(
        power_weight, power * jnp.bfloat16(-0.5), (((1,), (1,)), ((), ())), preferred_element_type=jnp.float32
    )
    score = score + jnp.take(log_prior, row_class)[None, :]
    best_score = lax.pmax(jnp.max(score, axis=1), "cls")

    capacity = max(2, 3 * local_rows // (dom_size * cls_size))
    slots = dom_size * capacity
    fact_class = every_fact[3].astype(jnp.float32).astype(jnp.int32) - dom_index * owned
    owned_here = (fact_class >= 0) & (fact_class < owned)
    running = jnp.cumsum(owned_here.astype(jnp.int32))
    slot_of = jnp.where(owned_here, running - 1, -1)
    slot_ids = jnp.arange(slots, dtype=jnp.int32)
    picker = (slot_ids[:, None] == slot_of[None, :]).astype(jnp.bfloat16)
    picked = lax.dot_general(
        every_fact, picker, (((1,), (1,)), ((), ())), preferred_element_type=jnp.float32
    )
    filled = slot_ids < running[-1]
    slot_defocus = jnp.where(filled, (picked[0] + picked[1]) + picked[2], 1.0)
    slot_pose = picked[3].astype(jnp.int32) - dom_index * owned
    slot_pose = jnp.where(filled, slot_pose * rotations + picked[4].astype(jnp.int32), -1)
    slot_power = power_rows(slot_defocus, inv_noise)
    own_poses = jnp.arange(owned * rotations, dtype=jnp.int32)
    gather_own = (own_poses[:, None] == slot_pose[None, :]).astype(jnp.bfloat16)
    denominator = jnp.dot(gather_own, slot_power, preferred_element_type=jnp.float32)

    class_images = numerator / (jnp.concatenate([denominator, denominator], axis=1) + 1.0)
    return best_score, class_images.reshape(owned, rotations, 2 * pixels)


def solution(mesh):
    dom_size, cls_size = mesh.devices.shape
    split = Mesh(mesh.devices.reshape(dom_size // 2, 2, cls_size), ("chip", "core", "cls"))
    dom = ("chip", "core")
    placed = (P(dom, None), P(dom), P(), P(("cls",) + dom, None, None), P(dom), P(dom), P())
    return jax.shard_map(
        on_device,
        mesh=split,
        in_specs=placed,
        out_specs=(P(dom), P(("cls",) + dom, None, None)),
        check_vma=False,
    )
```

```python
import math

import jax
import jax.numpy as jnp
from jax import lax
from jax.experimental import pallas as pl
from jax.sharding import Mesh, PartitionSpec as P

AMPLITUDE = math.hypot(0.995, 0.1)
PHASE = math.atan2(0.1, 0.995)
ROW_BLOCK = 128


def split_pieces(values, width):
    pieces = []
    rest = values
    for _ in range(3):
        piece = lax.reduce_precision(rest, exponent_bits=8, mantissa_bits=7)
        pieces.append(piece.astype(jnp.bfloat16))
        rest = rest - piece
    joined = jnp.concatenate(pieces, axis=1)
    return jnp.pad(joined, ((0, 0), (0, width - joined.shape[1])))


def contrast_tables(defocus, pixels):
    groups = pixels // 64
    scaled = 12.0 * defocus
    row_offset = (jnp.arange(groups, dtype=jnp.int32) - pixels // 128).astype(jnp.float32)
    row_angle = scaled[:, None] * (row_offset * row_offset / 4096.0)[None, :]
    column = (jnp.arange(128, dtype=jnp.int32) % 64).astype(jnp.float32)
    column_angle = scaled[:, None] * (column * column / 4096.0)[None, :] + PHASE
    width = -(-3 * groups // 128) * 128
    row_sin = split_pieces(-AMPLITUDE * jnp.sin(row_angle), width)
    row_cos = split_pieces(-AMPLITUDE * jnp.cos(row_angle), width)
    slot = jnp.arange(width, dtype=jnp.int32)[:, None]
    group_of = (jnp.arange(pixels, dtype=jnp.int32) // 64)[None, :]
    expand = ((slot < 3 * groups) & (slot % groups == group_of)).astype(jnp.bfloat16)
    return row_sin, row_cos, expand, jnp.cos(column_angle), jnp.sin(column_angle)


def contrast_tile(row_sin, row_cos, col_cos, col_sin, tile):
    lanes = slice(tile * 128, (tile + 1) * 128)
    return row_sin[:, lanes] * col_cos + row_cos[:, lanes] * col_sin


def weights_kernel(
    row_sin_ref, row_cos_ref, expand_ref, col_cos_ref, col_sin_ref, noise_ref, particles_ref, selector_ref,
    out_ref, power_ref, sums_ref, mine_ref,
):
    pixels = noise_ref.shape[1]
    row_sin = jnp.dot(row_sin_ref[...], expand_ref[...], preferred_element_type=jnp.float32)
    row_cos = jnp.dot(row_cos_ref[...], expand_ref[...], preferred_element_type=jnp.float32)
    col_cos = col_cos_ref[...]
    col_sin = col_sin_ref[...]
    for tile in range(pixels // 128):
        lanes = slice(tile * 128, (tile + 1) * 128)
        imag = slice(pixels + tile * 128, pixels + (tile + 1) * 128)
        contrast_rows = contrast_tile(row_sin, row_cos, col_cos, col_sin, tile)
        factor = noise_ref[:, lanes] * contrast_rows
        out_ref[:, lanes] = (particles_ref[:, lanes].astype(jnp.float32) * factor).astype(jnp.bfloat16)
        out_ref[:, imag] = (particles_ref[:, imag].astype(jnp.float32) * factor).astype(jnp.bfloat16)
        power_ref[:, lanes] = (factor * contrast_rows).astype(jnp.bfloat16)

    @pl.when(pl.program_id(0) == 0)
    def _():
        sums_ref[...] = jnp.zeros_like(sums_ref)
        mine_ref[...] = jnp.zeros_like(mine_ref)

    half = sums_ref.shape[0]
    sums_ref[...] += jnp.dot(selector_ref[:half, :], out_ref[...], preferred_element_type=jnp.float32)
    mine_ref[...] += jnp.dot(selector_ref[half:, :], out_ref[...], preferred_element_type=jnp.float32)


def power_kernel(row_sin_ref, row_cos_ref, expand_ref, col_cos_ref, col_sin_ref, noise_ref, power_ref):
    pixels = noise_ref.shape[1]
    row_sin = jnp.dot(row_sin_ref[...], expand_ref[...], preferred_element_type=jnp.float32)
    row_cos = jnp.dot(row_cos_ref[...], expand_ref[...], preferred_element_type=jnp.float32)
    col_cos = col_cos_ref[...]
    col_sin = col_sin_ref[...]
    for tile in range(pixels // 128):
        lanes = slice(tile * 128, (tile + 1) * 128)
        contrast_rows = contrast_tile(row_sin, row_cos, col_cos, col_sin, tile)
        factor = noise_ref[:, lanes] * contrast_rows
        power_ref[:, lanes] = (factor * contrast_rows).astype(jnp.bfloat16)


def table_specs(block, width, pixels):
    return [
        pl.BlockSpec((block, width), lambda i: (i, 0)),
        pl.BlockSpec((block, width), lambda i: (i, 0)),
        pl.BlockSpec((width, pixels), lambda i: (0, 0)),
        pl.BlockSpec((block, 128), lambda i: (i, 0)),
        pl.BlockSpec((block, 128), lambda i: (i, 0)),
        pl.BlockSpec((1, pixels), lambda i: (0, 0)),
    ]


def weighted_rows(particles, defocus, inv_noise, selector):
    rows = particles.shape[0]
    poses = selector.shape[0]
    pixels = inv_noise.shape[0]
    block = min(ROW_BLOCK, rows)
    tables = contrast_tables(defocus, pixels)
    width = tables[0].shape[1]
    return pl.pallas_call(
        weights_kernel,
        grid=(rows // block,),
        in_specs=table_specs(block, width, pixels)
        + [pl.BlockSpec((block, 2 * pixels), lambda i: (i, 0)), pl.BlockSpec((poses, block), lambda i: (0, i))],
        out_specs=[
            pl.BlockSpec((block, 2 * pixels), lambda i: (i, 0)),
            pl.BlockSpec((block, pixels), lambda i: (i, 0)),
            pl.BlockSpec((poses // 2, 2 * pixels), lambda i: (0, 0)),
            pl.BlockSpec((poses // 2, 2 * pixels), lambda i: (0, 0)),
        ],
        out_shape=[
            jax.ShapeDtypeStruct((rows, 2 * pixels), jnp.bfloat16),
            jax.ShapeDtypeStruct((rows, pixels), jnp.bfloat16),
            jax.ShapeDtypeStruct((poses // 2, 2 * pixels), jnp.float32),
            jax.ShapeDtypeStruct((poses // 2, 2 * pixels), jnp.float32),
        ],
    )(*tables, inv_noise[None, :], particles, selector)


def power_rows(defocus, inv_noise):
    rows = defocus.shape[0]
    pixels = inv_noise.shape[0]
    block = min(ROW_BLOCK, rows)
    tables = contrast_tables(defocus, pixels)
    width = tables[0].shape[1]
    return pl.pallas_call(
        power_kernel,
        grid=(rows // block,),
        in_specs=table_specs(block, width, pixels),
        out_specs=pl.BlockSpec((block, pixels), lambda i: (i, 0)),
        out_shape=jax.ShapeDtypeStruct((rows, pixels), jnp.bfloat16),
    )(*tables, inv_noise[None, :])


def on_device(particles, defocus, inv_noise, references, part_class, part_rot, counts):
    local_rows = particles.shape[0]
    pixels = inv_noise.shape[0]
    owned = references.shape[0]
    rotations = references.shape[1]
    chips = lax.axis_size("chip")
    dom_size = 2 * chips
    cls_size = lax.axis_size("cls")
    cls_index = lax.axis_index("cls")
    chip = lax.axis_index("chip")
    core = lax.axis_index("core")
    dom_index = 2 * chip + core
    block_classes = dom_size * owned
    block_first = cls_index * block_classes
    swap = [(0, 1), (1, 0)]

    local_class = part_class - block_first
    facts = split_pieces(defocus[None, :], 3 * local_rows).reshape(3, local_rows)
    block_class = jnp.clip(local_class, -1, block_classes).astype(jnp.bfloat16)
    facts = jnp.concatenate([facts, block_class[None, :], part_rot.astype(jnp.bfloat16)[None, :]], axis=0)
    ref_rows = owned * rotations
    extra_lanes = -(-facts.size // (ref_rows * 128)) * 128
    facts = jnp.pad(facts.reshape(-1), (0, extra_lanes * ref_rows - facts.size))
    sending = jnp.concatenate(
        [references.reshape(ref_rows, 2 * pixels), facts.reshape(ref_rows, extra_lanes)], axis=1
    )
    gathered = lax.all_gather(sending, ("chip", "core"), axis=0, tiled=False)
    flat_images = gathered[:, :, : 2 * pixels].reshape(block_classes * rotations, 2 * pixels)
    every_fact = gathered[:, :, 2 * pixels :].reshape(dom_size, -1)[:, : 5 * local_rows]
    row_class = block_first + jnp.arange(block_classes * rotations, dtype=jnp.int32) // rotations
    every_fact = every_fact.reshape(dom_size, 5, local_rows).transpose(1, 0, 2).reshape(5, dom_size * local_rows)
    real_part = flat_images[:, :pixels].astype(jnp.float32)
    imag_part = flat_images[:, pixels:].astype(jnp.float32)
    power = (real_part * real_part + imag_part * imag_part).astype(jnp.bfloat16)

    in_block = (local_class >= 0) & (local_class < block_classes)
    owner = local_class // owned
    mine = (owner % 2 == core).astype(jnp.int32)
    pose = ((mine * chips + owner // 2) * owned + local_class % owned) * rotations + part_rot
    pose = jnp.where(in_block, pose, -1)
    poses = jnp.arange(block_classes * rotations, dtype=jnp.int32)
    selector = (poses[:, None] == pose[None, :]).astype(jnp.bfloat16)
    weighted, power_weight, for_other, for_me = weighted_rows(particles, defocus, inv_noise, selector)
    chip_sums = for_me + lax.ppermute(for_other, "core", swap)
    numerator = lax.psum_scatter(chip_sums, "chip", scatter_dimension=0, tiled=True)

    class_total = counts.shape[0]
    log_prior = jnp.log(
        (counts + 1).astype(jnp.float32) / (jnp.sum(counts) + class_total).astype(jnp.float32)
    )
    score = lax.dot_general(
        weighted, flat_images, (((1,), (1,)), ((), ())), preferred_element_type=jnp.float32
    ) + lax.dot_general(
        power_weight, power * jnp.bfloat16(-0.5), (((1,), (1,)), ((), ())), preferred_element_type=jnp.float32
    )
    score = score + jnp.take(log_prior, row_class)[None, :]
    best_score = jnp.max(score, axis=1)
    step = 1
    while step < cls_size:
        pairs = [(c, c ^ step) for c in range(cls_size)]
        best_score = jnp.maximum(best_score, lax.ppermute(best_score, "cls", pairs))
        step *= 2

    capacity = max(2, 3 * local_rows // (dom_size * cls_size))
    slots = dom_size * capacity
    fact_class = every_fact[3].astype(jnp.float32).astype(jnp.int32) - dom_index * owned
    owned_here = (fact_class >= 0) & (fact_class < owned)
    running = jnp.cumsum(owned_here.astype(jnp.int32))
    slot_of = jnp.where(owned_here, running - 1, -1)
    slot_ids = jnp.arange(slots, dtype=jnp.int32)
    picker = (slot_ids[:, None] == slot_of[None, :]).astype(jnp.bfloat16)
    picked = lax.dot_general(
        every_fact, picker, (((1,), (1,)), ((), ())), preferred_element_type=jnp.float32
    )
    filled = slot_ids < running[-1]
    slot_defocus = jnp.where(filled, (picked[0] + picked[1]) + picked[2], 1.0)
    slot_pose = picked[3].astype(jnp.int32) - dom_index * owned
    slot_pose = jnp.where(filled, slot_pose * rotations + picked[4].astype(jnp.int32), -1)
    slot_power = power_rows(slot_defocus, inv_noise)
    own_poses = jnp.arange(owned * rotations, dtype=jnp.int32)
    gather_own = (own_poses[:, None] == slot_pose[None, :]).astype(jnp.bfloat16)
    denominator = jnp.dot(gather_own, slot_power, preferred_element_type=jnp.float32)

    class_images = numerator / (jnp.concatenate([denominator, denominator], axis=1) + 1.0)
    return best_score, class_images.reshape(owned, rotations, 2 * pixels)


def solution(mesh):
    dom_size, cls_size = mesh.devices.shape
    split = Mesh(mesh.devices.reshape(dom_size // 2, 2, cls_size), ("chip", "core", "cls"))
    dom = ("chip", "core")
    placed = (P(dom, None), P(dom), P(), P(("cls",) + dom, None, None), P(dom), P(dom), P())
    return jax.shard_map(
        on_device,
        mesh=split,
        in_specs=placed,
        out_specs=(P(dom), P(("cls",) + dom, None, None)),
        check_vma=False,
    )
```

```python
import math

import jax
import jax.numpy as jnp
from jax import lax
from jax.experimental import pallas as pl
from jax.sharding import Mesh, PartitionSpec as P

AMPLITUDE = math.hypot(0.995, 0.1)
PHASE = math.atan2(0.1, 0.995)
ROW_BLOCK = 128


def split_pieces(values, width):
    pieces = []
    rest = values
    for _ in range(3):
        piece = lax.reduce_precision(rest, exponent_bits=8, mantissa_bits=7)
        pieces.append(piece.astype(jnp.bfloat16))
        rest = rest - piece
    joined = jnp.concatenate(pieces, axis=1)
    return jnp.pad(joined, ((0, 0), (0, width - joined.shape[1])))


def contrast_tables(defocus, pixels):
    groups = pixels // 64
    scaled = 12.0 * defocus
    row_offset = (jnp.arange(groups, dtype=jnp.int32) - pixels // 128).astype(jnp.float32)
    row_angle = scaled[:, None] * (row_offset * row_offset / 4096.0)[None, :]
    column = (jnp.arange(128, dtype=jnp.int32) % 64).astype(jnp.float32)
    column_angle = scaled[:, None] * (column * column / 4096.0)[None, :] + PHASE
    width = -(-3 * groups // 128) * 128
    row_sin = split_pieces(-AMPLITUDE * jnp.sin(row_angle), width)
    row_cos = split_pieces(-AMPLITUDE * jnp.cos(row_angle), width)
    slot = jnp.arange(width, dtype=jnp.int32)[:, None]
    group_of = (jnp.arange(pixels, dtype=jnp.int32) // 64)[None, :]
    expand = ((slot < 3 * groups) & (slot % groups == group_of)).astype(jnp.bfloat16)
    return row_sin, row_cos, expand, jnp.cos(column_angle), jnp.sin(column_angle)


def contrast_tile(row_sin, row_cos, col_cos, col_sin, tile):
    lanes = slice(tile * 128, (tile + 1) * 128)
    return row_sin[:, lanes] * col_cos + row_cos[:, lanes] * col_sin


def weights_kernel(
    row_sin_ref, row_cos_ref, expand_ref, col_cos_ref, col_sin_ref, noise_ref, particles_ref, selector_ref,
    out_ref, power_ref, sums_ref, mine_ref,
):
    pixels = noise_ref.shape[1]
    row_sin = jnp.dot(row_sin_ref[...], expand_ref[...], preferred_element_type=jnp.float32)
    row_cos = jnp.dot(row_cos_ref[...], expand_ref[...], preferred_element_type=jnp.float32)
    col_cos = col_cos_ref[...]
    col_sin = col_sin_ref[...]
    for tile in range(pixels // 128):
        lanes = slice(tile * 128, (tile + 1) * 128)
        imag = slice(pixels + tile * 128, pixels + (tile + 1) * 128)
        contrast_rows = contrast_tile(row_sin, row_cos, col_cos, col_sin, tile)
        factor = noise_ref[:, lanes] * contrast_rows
        out_ref[:, lanes] = (particles_ref[:, lanes].astype(jnp.float32) * factor).astype(jnp.bfloat16)
        out_ref[:, imag] = (particles_ref[:, imag].astype(jnp.float32) * factor).astype(jnp.bfloat16)
        power_ref[:, lanes] = (factor * contrast_rows).astype(jnp.bfloat16)

    @pl.when(pl.program_id(0) == 0)
    def _():
        sums_ref[...] = jnp.zeros_like(sums_ref)
        mine_ref[...] = jnp.zeros_like(mine_ref)

    half = sums_ref.shape[0]
    sums_ref[...] += jnp.dot(selector_ref[:half, :], out_ref[...], preferred_element_type=jnp.float32)
    mine_ref[...] += jnp.dot(selector_ref[half:, :], out_ref[...], preferred_element_type=jnp.float32)


def power_kernel(row_sin_ref, row_cos_ref, expand_ref, col_cos_ref, col_sin_ref, noise_ref, power_ref):
    pixels = noise_ref.shape[1]
    row_sin = jnp.dot(row_sin_ref[...], expand_ref[...], preferred_element_type=jnp.float32)
    row_cos = jnp.dot(row_cos_ref[...], expand_ref[...], preferred_element_type=jnp.float32)
    col_cos = col_cos_ref[...]
    col_sin = col_sin_ref[...]
    for tile in range(pixels // 128):
        lanes = slice(tile * 128, (tile + 1) * 128)
        contrast_rows = contrast_tile(row_sin, row_cos, col_cos, col_sin, tile)
        factor = noise_ref[:, lanes] * contrast_rows
        power_ref[:, lanes] = (factor * contrast_rows).astype(jnp.bfloat16)


def table_specs(block, width, pixels):
    return [
        pl.BlockSpec((block, width), lambda i: (i, 0)),
        pl.BlockSpec((block, width), lambda i: (i, 0)),
        pl.BlockSpec((width, pixels), lambda i: (0, 0)),
        pl.BlockSpec((block, 128), lambda i: (i, 0)),
        pl.BlockSpec((block, 128), lambda i: (i, 0)),
        pl.BlockSpec((1, pixels), lambda i: (0, 0)),
    ]


def weighted_rows(particles, defocus, inv_noise, selector):
    rows = particles.shape[0]
    poses = selector.shape[0]
    pixels = inv_noise.shape[0]
    block = min(ROW_BLOCK, rows)
    tables = contrast_tables(defocus, pixels)
    width = tables[0].shape[1]
    return pl.pallas_call(
        weights_kernel,
        grid=(rows // block,),
        in_specs=table_specs(block, width, pixels)
        + [pl.BlockSpec((block, 2 * pixels), lambda i: (i, 0)), pl.BlockSpec((poses, block), lambda i: (0, i))],
        out_specs=[
            pl.BlockSpec((block, 2 * pixels), lambda i: (i, 0)),
            pl.BlockSpec((block, pixels), lambda i: (i, 0)),
            pl.BlockSpec((poses // 2, 2 * pixels), lambda i: (0, 0)),
            pl.BlockSpec((poses // 2, 2 * pixels), lambda i: (0, 0)),
        ],
        out_shape=[
            jax.ShapeDtypeStruct((rows, 2 * pixels), jnp.bfloat16),
            jax.ShapeDtypeStruct((rows, pixels), jnp.bfloat16),
            jax.ShapeDtypeStruct((poses // 2, 2 * pixels), jnp.float32),
            jax.ShapeDtypeStruct((poses // 2, 2 * pixels), jnp.float32),
        ],
    )(*tables, inv_noise[None, :], particles, selector)


def power_rows(defocus, inv_noise):
    rows = defocus.shape[0]
    pixels = inv_noise.shape[0]
    block = min(ROW_BLOCK, rows)
    tables = contrast_tables(defocus, pixels)
    width = tables[0].shape[1]
    return pl.pallas_call(
        power_kernel,
        grid=(rows // block,),
        in_specs=table_specs(block, width, pixels),
        out_specs=pl.BlockSpec((block, pixels), lambda i: (i, 0)),
        out_shape=jax.ShapeDtypeStruct((rows, pixels), jnp.bfloat16),
    )(*tables, inv_noise[None, :])


def on_device(particles, defocus, inv_noise, references, part_class, part_rot, counts):
    local_rows = particles.shape[0]
    pixels = inv_noise.shape[0]
    owned = references.shape[0]
    rotations = references.shape[1]
    chips = lax.axis_size("chip")
    dom_size = 2 * chips
    cls_size = lax.axis_size("cls")
    cls_index = lax.axis_index("cls")
    chip = lax.axis_index("chip")
    core = lax.axis_index("core")
    dom_index = 2 * chip + core
    block_classes = dom_size * owned
    block_first = cls_index * block_classes
    swap = [(0, 1), (1, 0)]

    local_class = part_class - block_first
    facts = split_pieces(defocus[None, :], 3 * local_rows).reshape(3, local_rows)
    block_class = jnp.clip(local_class, -1, block_classes).astype(jnp.bfloat16)
    facts = jnp.concatenate([facts, block_class[None, :], part_rot.astype(jnp.bfloat16)[None, :]], axis=0)
    ref_rows = owned * rotations
    extra_lanes = -(-facts.size // (ref_rows * 128)) * 128
    facts = jnp.pad(facts.reshape(-1), (0, extra_lanes * ref_rows - facts.size))
    sending = jnp.concatenate(
        [references.reshape(ref_rows, 2 * pixels), facts.reshape(ref_rows, extra_lanes)], axis=1
    )
    gathered = lax.all_gather(sending, ("chip", "core"), axis=0, tiled=False)
    flat_images = gathered[:, :, : 2 * pixels].reshape(block_classes * rotations, 2 * pixels)
    every_fact = gathered[:, :, 2 * pixels :].reshape(dom_size, -1)[:, : 5 * local_rows]
    row_class = block_first + jnp.arange(block_classes * rotations, dtype=jnp.int32) // rotations
    every_fact = every_fact.reshape(dom_size, 5, local_rows).transpose(1, 0, 2).reshape(5, dom_size * local_rows)
    real_part = flat_images[:, :pixels].astype(jnp.float32)
    imag_part = flat_images[:, pixels:].astype(jnp.float32)
    power = (real_part * real_part + imag_part * imag_part).astype(jnp.bfloat16)

    in_block = (local_class >= 0) & (local_class < block_classes)
    owner = local_class // owned
    mine = (owner % 2 == core).astype(jnp.int32)
    offset = (owner // 2 - chip) % chips
    pose = ((mine * chips + offset) * owned + local_class % owned) * rotations + part_rot
    pose = jnp.where(in_block, pose, -1)
    poses = jnp.arange(block_classes * rotations, dtype=jnp.int32)
    selector = (poses[:, None] == pose[None, :]).astype(jnp.bfloat16)
    weighted, power_weight, for_other, for_me = weighted_rows(particles, defocus, inv_noise, selector)
    chip_sums = (for_me + lax.ppermute(for_other, "core", swap)).reshape(chips, owned * rotations, 2 * pixels)
    numerator = chip_sums[0]
    for shift in range(1, chips):
        pairs = [(c, (c + shift) % chips) for c in range(chips)]
        arrived = lax.ppermute(chip_sums[shift].astype(jnp.bfloat16), "chip", pairs)
        numerator = numerator + arrived.astype(jnp.float32)

    class_total = counts.shape[0]
    log_prior = jnp.log(
        (counts + 1).astype(jnp.float32) / (jnp.sum(counts) + class_total).astype(jnp.float32)
    )
    score = lax.dot_general(
        weighted, flat_images, (((1,), (1,)), ((), ())), preferred_element_type=jnp.float32
    ) + lax.dot_general(
        power_weight, power * jnp.bfloat16(-0.5), (((1,), (1,)), ((), ())), preferred_element_type=jnp.float32
    )
    score = score + jnp.take(log_prior, row_class)[None, :]
    best_score = jnp.max(score, axis=1)
    step = 1
    while step < cls_size:
        pairs = [(c, c ^ step) for c in range(cls_size)]
        best_score = jnp.maximum(best_score, lax.ppermute(best_score, "cls", pairs))
        step *= 2

    capacity = max(2, 3 * local_rows // (dom_size * cls_size))
    slots = dom_size * capacity
    fact_class = every_fact[3].astype(jnp.float32).astype(jnp.int32) - dom_index * owned
    owned_here = (fact_class >= 0) & (fact_class < owned)
    running = jnp.cumsum(owned_here.astype(jnp.int32))
    slot_of = jnp.where(owned_here, running - 1, -1)
    slot_ids = jnp.arange(slots, dtype=jnp.int32)
    picker = (slot_ids[:, None] == slot_of[None, :]).astype(jnp.bfloat16)
    picked = lax.dot_general(
        every_fact, picker, (((1,), (1,)), ((), ())), preferred_element_type=jnp.float32
    )
    filled = slot_ids < running[-1]
    slot_defocus = jnp.where(filled, (picked[0] + picked[1]) + picked[2], 1.0)
    slot_pose = picked[3].astype(jnp.int32) - dom_index * owned
    slot_pose = jnp.where(filled, slot_pose * rotations + picked[4].astype(jnp.int32), -1)
    slot_power = power_rows(slot_defocus, inv_noise)
    own_poses = jnp.arange(owned * rotations, dtype=jnp.int32)
    gather_own = (own_poses[:, None] == slot_pose[None, :]).astype(jnp.bfloat16)
    denominator = jnp.dot(gather_own, slot_power, preferred_element_type=jnp.float32)

    class_images = numerator / (jnp.concatenate([denominator, denominator], axis=1) + 1.0)
    return best_score, class_images.reshape(owned, rotations, 2 * pixels)


def solution(mesh):
    dom_size, cls_size = mesh.devices.shape
    split = Mesh(mesh.devices.reshape(dom_size // 2, 2, cls_size), ("chip", "core", "cls"))
    dom = ("chip", "core")
    placed = (P(dom, None), P(dom), P(), P(("cls",) + dom, None, None), P(dom), P(dom), P())
    return jax.shard_map(
        on_device,
        mesh=split,
        in_specs=placed,
        out_specs=(P(dom), P(("cls",) + dom, None, None)),
        check_vma=False,
    )
```

```python
import math

import jax
import jax.numpy as jnp
from jax import lax
from jax.experimental import pallas as pl
from jax.sharding import Mesh, PartitionSpec as P

AMPLITUDE = math.hypot(0.995, 0.1)
PHASE = math.atan2(0.1, 0.995)
ROW_BLOCK = 128


def split_pieces(values, width):
    pieces = []
    rest = values
    for _ in range(3):
        piece = lax.reduce_precision(rest, exponent_bits=8, mantissa_bits=7)
        pieces.append(piece.astype(jnp.bfloat16))
        rest = rest - piece
    joined = jnp.concatenate(pieces, axis=1)
    return jnp.pad(joined, ((0, 0), (0, width - joined.shape[1])))


def contrast_tables(defocus, pixels):
    groups = pixels // 64
    scaled = 12.0 * defocus
    row_offset = (jnp.arange(groups, dtype=jnp.int32) - pixels // 128).astype(jnp.float32)
    row_angle = scaled[:, None] * (row_offset * row_offset / 4096.0)[None, :]
    column = (jnp.arange(128, dtype=jnp.int32) % 64).astype(jnp.float32)
    column_angle = scaled[:, None] * (column * column / 4096.0)[None, :] + PHASE
    width = -(-3 * groups // 128) * 128
    row_sin = split_pieces(-AMPLITUDE * jnp.sin(row_angle), width)
    row_cos = split_pieces(-AMPLITUDE * jnp.cos(row_angle), width)
    slot = jnp.arange(width, dtype=jnp.int32)[:, None]
    group_of = (jnp.arange(pixels, dtype=jnp.int32) // 64)[None, :]
    expand = ((slot < 3 * groups) & (slot % groups == group_of)).astype(jnp.bfloat16)
    return row_sin, row_cos, expand, jnp.cos(column_angle), jnp.sin(column_angle)


def contrast_tile(row_sin, row_cos, col_cos, col_sin, tile):
    lanes = slice(tile * 128, (tile + 1) * 128)
    return row_sin[:, lanes] * col_cos + row_cos[:, lanes] * col_sin


def make_weights_kernel(with_power):
    def weights_kernel(
        row_sin_ref, row_cos_ref, expand_ref, col_cos_ref, col_sin_ref, noise_ref, particles_ref, selector_ref,
        out_ref, *rest,
    ):
        if with_power:
            power_ref, other_ref, mine_ref = rest
        else:
            other_ref, mine_ref = rest
        pixels = noise_ref.shape[1]
        row_sin = jnp.dot(row_sin_ref[...], expand_ref[...], preferred_element_type=jnp.float32)
        row_cos = jnp.dot(row_cos_ref[...], expand_ref[...], preferred_element_type=jnp.float32)
        col_cos = col_cos_ref[...]
        col_sin = col_sin_ref[...]
        for tile in range(pixels // 128):
            lanes = slice(tile * 128, (tile + 1) * 128)
            contrast_rows = contrast_tile(row_sin, row_cos, col_cos, col_sin, tile)
            factor = noise_ref[:, lanes] * contrast_rows
            out_ref[:, lanes] = (particles_ref[:, lanes].astype(jnp.float32) * factor).astype(jnp.bfloat16)
            if with_power:
                power_ref[:, lanes] = (factor * contrast_rows).astype(jnp.bfloat16)

        @pl.when(pl.program_id(0) == 0)
        def _():
            other_ref[...] = jnp.zeros_like(other_ref)
            mine_ref[...] = jnp.zeros_like(mine_ref)

        half = other_ref.shape[0]
        other_ref[...] += jnp.dot(selector_ref[:half, :], out_ref[...], preferred_element_type=jnp.float32)
        mine_ref[...] += jnp.dot(selector_ref[half:, :], out_ref[...], preferred_element_type=jnp.float32)

    return weights_kernel


def power_kernel(row_sin_ref, row_cos_ref, expand_ref, col_cos_ref, col_sin_ref, noise_ref, power_ref):
    pixels = noise_ref.shape[1]
    row_sin = jnp.dot(row_sin_ref[...], expand_ref[...], preferred_element_type=jnp.float32)
    row_cos = jnp.dot(row_cos_ref[...], expand_ref[...], preferred_element_type=jnp.float32)
    col_cos = col_cos_ref[...]
    col_sin = col_sin_ref[...]
    for tile in range(pixels // 128):
        lanes = slice(tile * 128, (tile + 1) * 128)
        contrast_rows = contrast_tile(row_sin, row_cos, col_cos, col_sin, tile)
        factor = noise_ref[:, lanes] * contrast_rows
        power_ref[:, lanes] = (factor * contrast_rows).astype(jnp.bfloat16)


def table_specs(block, width, pixels):
    return [
        pl.BlockSpec((block, width), lambda i: (i, 0)),
        pl.BlockSpec((block, width), lambda i: (i, 0)),
        pl.BlockSpec((width, pixels), lambda i: (0, 0)),
        pl.BlockSpec((block, 128), lambda i: (i, 0)),
        pl.BlockSpec((block, 128), lambda i: (i, 0)),
        pl.BlockSpec((1, pixels), lambda i: (0, 0)),
    ]


def weighted_half(particles, tables, inv_noise, selector, part):
    rows = particles.shape[0]
    pixels = inv_noise.shape[0]
    poses = selector.shape[0]
    block = min(ROW_BLOCK, rows)
    width = tables[0].shape[1]
    with_power = part == 0
    outs = [pl.BlockSpec((block, pixels), lambda i: (i, 0))]
    shapes = [jax.ShapeDtypeStruct((rows, pixels), jnp.bfloat16)]
    if with_power:
        outs.append(pl.BlockSpec((block, pixels), lambda i: (i, 0)))
        shapes.append(jax.ShapeDtypeStruct((rows, pixels), jnp.bfloat16))
    for _ in range(2):
        outs.append(pl.BlockSpec((poses // 2, pixels), lambda i: (0, 0)))
        shapes.append(jax.ShapeDtypeStruct((poses // 2, pixels), jnp.float32))
    return pl.pallas_call(
        make_weights_kernel(with_power),
        grid=(rows // block,),
        in_specs=table_specs(block, width, pixels)
        + [pl.BlockSpec((block, pixels), lambda i: (i, part)), pl.BlockSpec((poses, block), lambda i: (0, i))],
        out_specs=outs,
        out_shape=shapes,
    )(*tables, inv_noise[None, :], particles, selector)


def power_rows(defocus, inv_noise):
    rows = defocus.shape[0]
    pixels = inv_noise.shape[0]
    block = min(ROW_BLOCK, rows)
    tables = contrast_tables(defocus, pixels)
    width = tables[0].shape[1]
    return pl.pallas_call(
        power_kernel,
        grid=(rows // block,),
        in_specs=table_specs(block, width, pixels),
        out_specs=pl.BlockSpec((block, pixels), lambda i: (i, 0)),
        out_shape=jax.ShapeDtypeStruct((rows, pixels), jnp.bfloat16),
    )(*tables, inv_noise[None, :])


def on_device(particles, defocus, inv_noise, references, part_class, part_rot, counts):
    local_rows = particles.shape[0]
    pixels = inv_noise.shape[0]
    owned = references.shape[0]
    rotations = references.shape[1]
    chips = lax.axis_size("chip")
    dom_size = 2 * chips
    cls_size = lax.axis_size("cls")
    cls_index = lax.axis_index("cls")
    chip = lax.axis_index("chip")
    core = lax.axis_index("core")
    dom_index = 2 * chip + core
    block_classes = dom_size * owned
    block_first = cls_index * block_classes
    swap = [(0, 1), (1, 0)]

    local_class = part_class - block_first
    facts = split_pieces(defocus[None, :], 3 * local_rows).reshape(3, local_rows)
    block_class = jnp.clip(local_class, -1, block_classes).astype(jnp.bfloat16)
    facts = jnp.concatenate([facts, block_class[None, :], part_rot.astype(jnp.bfloat16)[None, :]], axis=0)
    ref_rows = owned * rotations
    extra_lanes = -(-facts.size // (ref_rows * 128)) * 128
    facts = jnp.pad(facts.reshape(-1), (0, extra_lanes * ref_rows - facts.size))
    sending = jnp.concatenate(
        [references.reshape(ref_rows, 2 * pixels), facts.reshape(ref_rows, extra_lanes)], axis=1
    )
    gathered = lax.all_gather(sending, ("chip", "core"), axis=0, tiled=False)
    flat_images = gathered[:, :, : 2 * pixels].reshape(block_classes * rotations, 2 * pixels)
    every_fact = gathered[:, :, 2 * pixels :].reshape(dom_size, -1)[:, : 5 * local_rows]
    row_class = block_first + jnp.arange(block_classes * rotations, dtype=jnp.int32) // rotations
    every_fact = every_fact.reshape(dom_size, 5, local_rows).transpose(1, 0, 2).reshape(5, dom_size * local_rows)
    real_part = flat_images[:, :pixels].astype(jnp.float32)
    imag_part = flat_images[:, pixels:].astype(jnp.float32)
    power = (real_part * real_part + imag_part * imag_part).astype(jnp.bfloat16)

    in_block = (local_class >= 0) & (local_class < block_classes)
    owner = local_class // owned
    mine = (owner % 2 == core).astype(jnp.int32)
    pose = ((mine * chips + owner // 2) * owned + local_class % owned) * rotations + part_rot
    pose = jnp.where(in_block, pose, -1)
    poses = jnp.arange(block_classes * rotations, dtype=jnp.int32)
    selector = (poses[:, None] == pose[None, :]).astype(jnp.bfloat16)
    tables = contrast_tables(defocus, pixels)
    halves = []
    weighted_parts = []
    for part in range(2):
        made = weighted_half(particles, tables, inv_noise, selector, part)
        if part == 0:
            power_weight = made[1]
        weighted_parts.append(made[0])
        chip_sums = made[-1] + lax.ppermute(made[-2], "core", swap)
        halves.append(lax.psum_scatter(chip_sums, "chip", scatter_dimension=0, tiled=True))
    numerator = jnp.concatenate(halves, axis=1)

    class_total = counts.shape[0]
    log_prior = jnp.log(
        (counts + 1).astype(jnp.float32) / (jnp.sum(counts) + class_total).astype(jnp.float32)
    )
    score = lax.dot_general(
        weighted_parts[0], flat_images[:, :pixels], (((1,), (1,)), ((), ())), preferred_element_type=jnp.float32
    ) + lax.dot_general(
        weighted_parts[1], flat_images[:, pixels:], (((1,), (1,)), ((), ())), preferred_element_type=jnp.float32
    ) + lax.dot_general(
        power_weight, power * jnp.bfloat16(-0.5), (((1,), (1,)), ((), ())), preferred_element_type=jnp.float32
    )
    score = score + jnp.take(log_prior, row_class)[None, :]
    best_score = jnp.max(score, axis=1)
    step = 1
    while step < cls_size:
        pairs = [(c, c ^ step) for c in range(cls_size)]
        best_score = jnp.maximum(best_score, lax.ppermute(best_score, "cls", pairs))
        step *= 2

    capacity = max(2, 3 * local_rows // (dom_size * cls_size))
    slots = dom_size * capacity
    fact_class = every_fact[3].astype(jnp.float32).astype(jnp.int32) - dom_index * owned
    owned_here = (fact_class >= 0) & (fact_class < owned)
    running = jnp.cumsum(owned_here.astype(jnp.int32))
    slot_of = jnp.where(owned_here, running - 1, -1)
    slot_ids = jnp.arange(slots, dtype=jnp.int32)
    picker = (slot_ids[:, None] == slot_of[None, :]).astype(jnp.bfloat16)
    picked = lax.dot_general(
        every_fact, picker, (((1,), (1,)), ((), ())), preferred_element_type=jnp.float32
    )
    filled = slot_ids < running[-1]
    slot_defocus = jnp.where(filled, (picked[0] + picked[1]) + picked[2], 1.0)
    slot_pose = picked[3].astype(jnp.int32) - dom_index * owned
    slot_pose = jnp.where(filled, slot_pose * rotations + picked[4].astype(jnp.int32), -1)
    slot_power = power_rows(slot_defocus, inv_noise)
    own_poses = jnp.arange(owned * rotations, dtype=jnp.int32)
    gather_own = (own_poses[:, None] == slot_pose[None, :]).astype(jnp.bfloat16)
    denominator = jnp.dot(gather_own, slot_power, preferred_element_type=jnp.float32)

    class_images = numerator / (jnp.concatenate([denominator, denominator], axis=1) + 1.0)
    return best_score, class_images.reshape(owned, rotations, 2 * pixels)


def solution(mesh):
    dom_size, cls_size = mesh.devices.shape
    split = Mesh(mesh.devices.reshape(dom_size // 2, 2, cls_size), ("chip", "core", "cls"))
    dom = ("chip", "core")
    placed = (P(dom, None), P(dom), P(), P(("cls",) + dom, None, None), P(dom), P(dom), P())
    return jax.shard_map(
        on_device,
        mesh=split,
        in_specs=placed,
        out_specs=(P(dom), P(("cls",) + dom, None, None)),
        check_vma=False,
    )
```

```python
import math

import jax
import jax.numpy as jnp
from jax import lax
from jax.experimental import pallas as pl
from jax.sharding import Mesh, PartitionSpec as P

AMPLITUDE = math.hypot(0.995, 0.1)
PHASE = math.atan2(0.1, 0.995)
ROW_BLOCK = 128


def split_pieces(values, width):
    pieces = []
    rest = values
    for _ in range(3):
        piece = lax.reduce_precision(rest, exponent_bits=8, mantissa_bits=7)
        pieces.append(piece.astype(jnp.bfloat16))
        rest = rest - piece
    joined = jnp.concatenate(pieces, axis=1)
    return jnp.pad(joined, ((0, 0), (0, width - joined.shape[1])))


def contrast_tables(defocus, pixels):
    groups = pixels // 64
    scaled = 12.0 * defocus
    row_offset = (jnp.arange(groups, dtype=jnp.int32) - pixels // 128).astype(jnp.float32)
    row_angle = scaled[:, None] * (row_offset * row_offset / 4096.0)[None, :]
    column = (jnp.arange(128, dtype=jnp.int32) % 64).astype(jnp.float32)
    column_angle = scaled[:, None] * (column * column / 4096.0)[None, :] + PHASE
    width = -(-3 * groups // 128) * 128
    row_sin = split_pieces(-AMPLITUDE * jnp.sin(row_angle), width)
    row_cos = split_pieces(-AMPLITUDE * jnp.cos(row_angle), width)
    slot = jnp.arange(width, dtype=jnp.int32)[:, None]
    group_of = (jnp.arange(pixels, dtype=jnp.int32) // 64)[None, :]
    expand = ((slot < 3 * groups) & (slot % groups == group_of)).astype(jnp.bfloat16)
    return row_sin, row_cos, expand, jnp.cos(column_angle), jnp.sin(column_angle)


def contrast_tile(row_sin, row_cos, col_cos, col_sin, tile):
    lanes = slice(tile * 128, (tile + 1) * 128)
    return row_sin[:, lanes] * col_cos + row_cos[:, lanes] * col_sin


def weights_kernel(
    row_sin_ref, row_cos_ref, expand_ref, col_cos_ref, col_sin_ref, noise_ref, particles_ref, selector_ref,
    out_ref, power_ref, sums_ref, mine_ref,
):
    pixels = noise_ref.shape[1]
    row_sin_pieces = row_sin_ref[...]
    row_cos_pieces = row_cos_ref[...]
    col_cos = col_cos_ref[...]
    col_sin = col_sin_ref[...]
    for tile in range(pixels // 128):
        lanes = slice(tile * 128, (tile + 1) * 128)
        imag = slice(pixels + tile * 128, pixels + (tile + 1) * 128)
        expand = expand_ref[:, lanes]
        row_sin = jnp.dot(row_sin_pieces, expand, preferred_element_type=jnp.float32)
        row_cos = jnp.dot(row_cos_pieces, expand, preferred_element_type=jnp.float32)
        contrast_rows = row_sin * col_cos + row_cos * col_sin
        factor = noise_ref[:, lanes] * contrast_rows
        out_ref[:, lanes] = (particles_ref[:, lanes].astype(jnp.float32) * factor).astype(jnp.bfloat16)
        out_ref[:, imag] = (particles_ref[:, imag].astype(jnp.float32) * factor).astype(jnp.bfloat16)
        power_ref[:, lanes] = (factor * contrast_rows).astype(jnp.bfloat16)

    @pl.when(pl.program_id(0) == 0)
    def _():
        sums_ref[...] = jnp.zeros_like(sums_ref)
        mine_ref[...] = jnp.zeros_like(mine_ref)

    half = sums_ref.shape[0]
    sums_ref[...] += jnp.dot(selector_ref[:half, :], out_ref[...], preferred_element_type=jnp.float32)
    mine_ref[...] += jnp.dot(selector_ref[half:, :], out_ref[...], preferred_element_type=jnp.float32)


def power_kernel(row_sin_ref, row_cos_ref, expand_ref, col_cos_ref, col_sin_ref, noise_ref, power_ref):
    pixels = noise_ref.shape[1]
    row_sin = jnp.dot(row_sin_ref[...], expand_ref[...], preferred_element_type=jnp.float32)
    row_cos = jnp.dot(row_cos_ref[...], expand_ref[...], preferred_element_type=jnp.float32)
    col_cos = col_cos_ref[...]
    col_sin = col_sin_ref[...]
    for tile in range(pixels // 128):
        lanes = slice(tile * 128, (tile + 1) * 128)
        contrast_rows = contrast_tile(row_sin, row_cos, col_cos, col_sin, tile)
        factor = noise_ref[:, lanes] * contrast_rows
        power_ref[:, lanes] = (factor * contrast_rows).astype(jnp.bfloat16)


def table_specs(block, width, pixels):
    return [
        pl.BlockSpec((block, width), lambda i: (i, 0)),
        pl.BlockSpec((block, width), lambda i: (i, 0)),
        pl.BlockSpec((width, pixels), lambda i: (0, 0)),
        pl.BlockSpec((block, 128), lambda i: (i, 0)),
        pl.BlockSpec((block, 128), lambda i: (i, 0)),
        pl.BlockSpec((1, pixels), lambda i: (0, 0)),
    ]


def weighted_rows(particles, defocus, inv_noise, selector):
    rows = particles.shape[0]
    poses = selector.shape[0]
    pixels = inv_noise.shape[0]
    block = min(ROW_BLOCK, rows)
    tables = contrast_tables(defocus, pixels)
    width = tables[0].shape[1]
    return pl.pallas_call(
        weights_kernel,
        grid=(rows // block,),
        in_specs=table_specs(block, width, pixels)
        + [pl.BlockSpec((block, 2 * pixels), lambda i: (i, 0)), pl.BlockSpec((poses, block), lambda i: (0, i))],
        out_specs=[
            pl.BlockSpec((block, 2 * pixels), lambda i: (i, 0)),
            pl.BlockSpec((block, pixels), lambda i: (i, 0)),
            pl.BlockSpec((poses // 2, 2 * pixels), lambda i: (0, 0)),
            pl.BlockSpec((poses // 2, 2 * pixels), lambda i: (0, 0)),
        ],
        out_shape=[
            jax.ShapeDtypeStruct((rows, 2 * pixels), jnp.bfloat16),
            jax.ShapeDtypeStruct((rows, pixels), jnp.bfloat16),
            jax.ShapeDtypeStruct((poses // 2, 2 * pixels), jnp.float32),
            jax.ShapeDtypeStruct((poses // 2, 2 * pixels), jnp.float32),
        ],
    )(*tables, inv_noise[None, :], particles, selector)


def power_rows(defocus, inv_noise):
    rows = defocus.shape[0]
    pixels = inv_noise.shape[0]
    block = min(ROW_BLOCK, rows)
    tables = contrast_tables(defocus, pixels)
    width = tables[0].shape[1]
    return pl.pallas_call(
        power_kernel,
        grid=(rows // block,),
        in_specs=table_specs(block, width, pixels),
        out_specs=pl.BlockSpec((block, pixels), lambda i: (i, 0)),
        out_shape=jax.ShapeDtypeStruct((rows, pixels), jnp.bfloat16),
    )(*tables, inv_noise[None, :])


def on_device(particles, defocus, inv_noise, references, part_class, part_rot, counts):
    local_rows = particles.shape[0]
    pixels = inv_noise.shape[0]
    owned = references.shape[0]
    rotations = references.shape[1]
    chips = lax.axis_size("chip")
    dom_size = 2 * chips
    cls_size = lax.axis_size("cls")
    cls_index = lax.axis_index("cls")
    chip = lax.axis_index("chip")
    core = lax.axis_index("core")
    dom_index = 2 * chip + core
    block_classes = dom_size * owned
    block_first = cls_index * block_classes
    swap = [(0, 1), (1, 0)]

    local_class = part_class - block_first
    facts = split_pieces(defocus[None, :], 3 * local_rows).reshape(3, local_rows)
    block_class = jnp.clip(local_class, -1, block_classes).astype(jnp.bfloat16)
    facts = jnp.concatenate([facts, block_class[None, :], part_rot.astype(jnp.bfloat16)[None, :]], axis=0)
    ref_rows = owned * rotations
    extra_lanes = -(-facts.size // (ref_rows * 128)) * 128
    facts = jnp.pad(facts.reshape(-1), (0, extra_lanes * ref_rows - facts.size))
    sending = jnp.concatenate(
        [references.reshape(ref_rows, 2 * pixels), facts.reshape(ref_rows, extra_lanes)], axis=1
    )
    gathered = lax.all_gather(sending, ("chip", "core"), axis=0, tiled=False)
    flat_images = gathered[:, :, : 2 * pixels].reshape(block_classes * rotations, 2 * pixels)
    every_fact = gathered[:, :, 2 * pixels :].reshape(dom_size, -1)[:, : 5 * local_rows]
    row_class = block_first + jnp.arange(block_classes * rotations, dtype=jnp.int32) // rotations
    every_fact = every_fact.reshape(dom_size, 5, local_rows).transpose(1, 0, 2).reshape(5, dom_size * local_rows)
    real_part = flat_images[:, :pixels].astype(jnp.float32)
    imag_part = flat_images[:, pixels:].astype(jnp.float32)
    power = (real_part * real_part + imag_part * imag_part).astype(jnp.bfloat16)

    in_block = (local_class >= 0) & (local_class < block_classes)
    owner = local_class // owned
    mine = (owner % 2 == core).astype(jnp.int32)
    pose = ((mine * chips + owner // 2) * owned + local_class % owned) * rotations + part_rot
    pose = jnp.where(in_block, pose, -1)
    poses = jnp.arange(block_classes * rotations, dtype=jnp.int32)
    selector = (poses[:, None] == pose[None, :]).astype(jnp.bfloat16)
    weighted, power_weight, for_other, for_me = weighted_rows(particles, defocus, inv_noise, selector)
    chip_sums = for_me + lax.ppermute(for_other, "core", swap)
    numerator = lax.psum_scatter(chip_sums, "chip", scatter_dimension=0, tiled=True)

    class_total = counts.shape[0]
    log_prior = jnp.log(
        (counts + 1).astype(jnp.float32) / (jnp.sum(counts) + class_total).astype(jnp.float32)
    )
    score = lax.dot_general(
        weighted, flat_images, (((1,), (1,)), ((), ())), preferred_element_type=jnp.float32
    ) + lax.dot_general(
        power_weight, power * jnp.bfloat16(-0.5), (((1,), (1,)), ((), ())), preferred_element_type=jnp.float32
    )
    score = score + jnp.take(log_prior, row_class)[None, :]
    best_score = jnp.max(score, axis=1)
    step = 1
    while step < cls_size:
        pairs = [(c, c ^ step) for c in range(cls_size)]
        best_score = jnp.maximum(best_score, lax.ppermute(best_score, "cls", pairs))
        step *= 2

    capacity = max(2, 3 * local_rows // (dom_size * cls_size))
    slots = dom_size * capacity
    fact_class = every_fact[3].astype(jnp.float32).astype(jnp.int32) - dom_index * owned
    owned_here = (fact_class >= 0) & (fact_class < owned)
    running = jnp.cumsum(owned_here.astype(jnp.int32))
    slot_of = jnp.where(owned_here, running - 1, -1)
    slot_ids = jnp.arange(slots, dtype=jnp.int32)
    picker = (slot_ids[:, None] == slot_of[None, :]).astype(jnp.bfloat16)
    picked = lax.dot_general(
        every_fact, picker, (((1,), (1,)), ((), ())), preferred_element_type=jnp.float32
    )
    filled = slot_ids < running[-1]
    slot_defocus = jnp.where(filled, (picked[0] + picked[1]) + picked[2], 1.0)
    slot_pose = picked[3].astype(jnp.int32) - dom_index * owned
    slot_pose = jnp.where(filled, slot_pose * rotations + picked[4].astype(jnp.int32), -1)
    slot_power = power_rows(slot_defocus, inv_noise)
    own_poses = jnp.arange(owned * rotations, dtype=jnp.int32)
    gather_own = (own_poses[:, None] == slot_pose[None, :]).astype(jnp.bfloat16)
    denominator = jnp.dot(gather_own, slot_power, preferred_element_type=jnp.float32)

    class_images = numerator / (jnp.concatenate([denominator, denominator], axis=1) + 1.0)
    return best_score, class_images.reshape(owned, rotations, 2 * pixels)


def solution(mesh):
    dom_size, cls_size = mesh.devices.shape
    split = Mesh(mesh.devices.reshape(dom_size // 2, 2, cls_size), ("chip", "core", "cls"))
    dom = ("chip", "core")
    placed = (P(dom, None), P(dom), P(), P(("cls",) + dom, None, None), P(dom), P(dom), P())
    return jax.shard_map(
        on_device,
        mesh=split,
        in_specs=placed,
        out_specs=(P(dom), P(("cls",) + dom, None, None)),
        check_vma=False,
    )
```

```python
import math

import jax
import jax.numpy as jnp
from jax import lax
from jax.experimental import pallas as pl
from jax.sharding import Mesh, PartitionSpec as P

AMPLITUDE = math.hypot(0.995, 0.1)
PHASE = math.atan2(0.1, 0.995)
ROW_BLOCK = 128


def split_pieces(values, width):
    pieces = []
    rest = values
    for _ in range(3):
        piece = lax.reduce_precision(rest, exponent_bits=8, mantissa_bits=7)
        pieces.append(piece.astype(jnp.bfloat16))
        rest = rest - piece
    joined = jnp.concatenate(pieces, axis=1)
    return jnp.pad(joined, ((0, 0), (0, width - joined.shape[1])))


def contrast_tables(defocus, pixels):
    groups = pixels // 64
    scaled = 12.0 * defocus
    row_offset = (jnp.arange(groups, dtype=jnp.int32) - pixels // 128).astype(jnp.float32)
    row_angle = scaled[:, None] * (row_offset * row_offset / 4096.0)[None, :]
    column = jnp.arange(64, dtype=jnp.int32).astype(jnp.float32)
    column_angle = scaled[:, None] * (column * column / 4096.0)[None, :] + PHASE
    width = -(-3 * groups // 128) * 128
    row_sin = split_pieces(-AMPLITUDE * jnp.sin(row_angle), width)
    row_cos = split_pieces(-AMPLITUDE * jnp.cos(row_angle), width)
    slot = jnp.arange(width, dtype=jnp.int32)[:, None]
    group_of = (jnp.arange(pixels, dtype=jnp.int32) // 64)[None, :]
    expand = ((slot < 3 * groups) & (slot % groups == group_of)).astype(jnp.bfloat16)
    col_cos = jnp.cos(column_angle)
    col_sin = jnp.sin(column_angle)
    return row_sin, row_cos, expand, jnp.concatenate([col_cos, col_cos], 1), jnp.concatenate([col_sin, col_sin], 1)


def contrast_tile(row_sin, row_cos, col_cos, col_sin, tile):
    lanes = slice(tile * 128, (tile + 1) * 128)
    return row_sin[:, lanes] * col_cos + row_cos[:, lanes] * col_sin


def weights_kernel(
    row_sin_ref, row_cos_ref, expand_ref, col_cos_ref, col_sin_ref, noise_ref, particles_ref, selector_ref,
    out_ref, power_ref, sums_ref, mine_ref,
):
    pixels = noise_ref.shape[1]
    row_sin_pieces = row_sin_ref[...]
    row_cos_pieces = row_cos_ref[...]
    col_cos = col_cos_ref[...]
    col_sin = col_sin_ref[...]
    for tile in range(pixels // 128):
        lanes = slice(tile * 128, (tile + 1) * 128)
        imag = slice(pixels + tile * 128, pixels + (tile + 1) * 128)
        expand = expand_ref[:, lanes]
        row_sin = jnp.dot(row_sin_pieces, expand, preferred_element_type=jnp.float32)
        row_cos = jnp.dot(row_cos_pieces, expand, preferred_element_type=jnp.float32)
        contrast_rows = row_sin * col_cos + row_cos * col_sin
        factor = noise_ref[:, lanes] * contrast_rows
        out_ref[:, lanes] = (particles_ref[:, lanes].astype(jnp.float32) * factor).astype(jnp.bfloat16)
        out_ref[:, imag] = (particles_ref[:, imag].astype(jnp.float32) * factor).astype(jnp.bfloat16)
        power_ref[:, lanes] = (factor * contrast_rows).astype(jnp.bfloat16)

    @pl.when(pl.program_id(0) == 0)
    def _():
        sums_ref[...] = jnp.zeros_like(sums_ref)
        mine_ref[...] = jnp.zeros_like(mine_ref)

    half = sums_ref.shape[0]
    sums_ref[...] += jnp.dot(selector_ref[:half, :], out_ref[...], preferred_element_type=jnp.float32)
    mine_ref[...] += jnp.dot(selector_ref[half:, :], out_ref[...], preferred_element_type=jnp.float32)


def power_kernel(row_sin_ref, row_cos_ref, expand_ref, col_cos_ref, col_sin_ref, noise_ref, power_ref):
    pixels = noise_ref.shape[1]
    row_sin = jnp.dot(row_sin_ref[...], expand_ref[...], preferred_element_type=jnp.float32)
    row_cos = jnp.dot(row_cos_ref[...], expand_ref[...], preferred_element_type=jnp.float32)
    col_cos = col_cos_ref[...]
    col_sin = col_sin_ref[...]
    for tile in range(pixels // 128):
        lanes = slice(tile * 128, (tile + 1) * 128)
        contrast_rows = contrast_tile(row_sin, row_cos, col_cos, col_sin, tile)
        factor = noise_ref[:, lanes] * contrast_rows
        power_ref[:, lanes] = (factor * contrast_rows).astype(jnp.bfloat16)


def table_specs(block, width, pixels):
    return [
        pl.BlockSpec((block, width), lambda i: (i, 0)),
        pl.BlockSpec((block, width), lambda i: (i, 0)),
        pl.BlockSpec((width, pixels), lambda i: (0, 0)),
        pl.BlockSpec((block, 128), lambda i: (i, 0)),
        pl.BlockSpec((block, 128), lambda i: (i, 0)),
        pl.BlockSpec((1, pixels), lambda i: (0, 0)),
    ]


def weighted_rows(particles, defocus, inv_noise, selector):
    rows = particles.shape[0]
    poses = selector.shape[0]
    pixels = inv_noise.shape[0]
    block = min(2 * ROW_BLOCK if poses * pixels * 8 <= 16 * 2**20 else ROW_BLOCK, rows)
    tables = contrast_tables(defocus, pixels)
    width = tables[0].shape[1]
    return pl.pallas_call(
        weights_kernel,
        grid=(rows // block,),
        in_specs=table_specs(block, width, pixels)
        + [pl.BlockSpec((block, 2 * pixels), lambda i: (i, 0)), pl.BlockSpec((poses, block), lambda i: (0, i))],
        out_specs=[
            pl.BlockSpec((block, 2 * pixels), lambda i: (i, 0)),
            pl.BlockSpec((block, pixels), lambda i: (i, 0)),
            pl.BlockSpec((poses // 2, 2 * pixels), lambda i: (0, 0)),
            pl.BlockSpec((poses // 2, 2 * pixels), lambda i: (0, 0)),
        ],
        out_shape=[
            jax.ShapeDtypeStruct((rows, 2 * pixels), jnp.bfloat16),
            jax.ShapeDtypeStruct((rows, pixels), jnp.bfloat16),
            jax.ShapeDtypeStruct((poses // 2, 2 * pixels), jnp.float32),
            jax.ShapeDtypeStruct((poses // 2, 2 * pixels), jnp.float32),
        ],
    )(*tables, inv_noise[None, :], particles, selector)


def power_rows(defocus, inv_noise):
    rows = defocus.shape[0]
    pixels = inv_noise.shape[0]
    block = min(ROW_BLOCK, rows)
    tables = contrast_tables(defocus, pixels)
    width = tables[0].shape[1]
    return pl.pallas_call(
        power_kernel,
        grid=(rows // block,),
        in_specs=table_specs(block, width, pixels),
        out_specs=pl.BlockSpec((block, pixels), lambda i: (i, 0)),
        out_shape=jax.ShapeDtypeStruct((rows, pixels), jnp.bfloat16),
    )(*tables, inv_noise[None, :])


def on_device(particles, defocus, inv_noise, references, part_class, part_rot, counts):
    local_rows = particles.shape[0]
    pixels = inv_noise.shape[0]
    owned = references.shape[0]
    rotations = references.shape[1]
    chips = lax.axis_size("chip")
    dom_size = 2 * chips
    cls_size = lax.axis_size("cls")
    cls_index = lax.axis_index("cls")
    chip = lax.axis_index("chip")
    core = lax.axis_index("core")
    dom_index = 2 * chip + core
    block_classes = dom_size * owned
    block_first = cls_index * block_classes
    swap = [(0, 1), (1, 0)]

    local_class = part_class - block_first
    facts = split_pieces(defocus[None, :], 3 * local_rows).reshape(3, local_rows)
    block_class = jnp.clip(local_class, -1, block_classes).astype(jnp.bfloat16)
    facts = jnp.concatenate([facts, block_class[None, :], part_rot.astype(jnp.bfloat16)[None, :]], axis=0)
    ref_rows = owned * rotations
    extra_lanes = -(-facts.size // (ref_rows * 128)) * 128
    facts = jnp.pad(facts.reshape(-1), (0, extra_lanes * ref_rows - facts.size))
    sending = jnp.concatenate(
        [references.reshape(ref_rows, 2 * pixels), facts.reshape(ref_rows, extra_lanes)], axis=1
    )
    gathered = lax.all_gather(sending, ("chip", "core"), axis=0, tiled=False)
    flat_images = gathered[:, :, : 2 * pixels].reshape(block_classes * rotations, 2 * pixels)
    every_fact = gathered[:, :, 2 * pixels :].reshape(dom_size, -1)[:, : 5 * local_rows]
    row_class = block_first + jnp.arange(block_classes * rotations, dtype=jnp.int32) // rotations
    every_fact = every_fact.reshape(dom_size, 5, local_rows).transpose(1, 0, 2).reshape(5, dom_size * local_rows)
    real_part = flat_images[:, :pixels].astype(jnp.float32)
    imag_part = flat_images[:, pixels:].astype(jnp.float32)
    power = (real_part * real_part + imag_part * imag_part).astype(jnp.bfloat16)

    in_block = (local_class >= 0) & (local_class < block_classes)
    owner = local_class // owned
    mine = (owner % 2 == core).astype(jnp.int32)
    pose = ((mine * chips + owner // 2) * owned + local_class % owned) * rotations + part_rot
    pose = jnp.where(in_block, pose, -1)
    poses = jnp.arange(block_classes * rotations, dtype=jnp.int32)
    selector = (poses[:, None] == pose[None, :]).astype(jnp.bfloat16)
    weighted, power_weight, for_other, for_me = weighted_rows(particles, defocus, inv_noise, selector)
    chip_sums = for_me + lax.ppermute(for_other, "core", swap)
    numerator = lax.psum_scatter(chip_sums, "chip", scatter_dimension=0, tiled=True)

    class_total = counts.shape[0]
    log_prior = jnp.log(
        (counts + 1).astype(jnp.float32) / (jnp.sum(counts) + class_total).astype(jnp.float32)
    )
    score = lax.dot_general(
        weighted, flat_images, (((1,), (1,)), ((), ())), preferred_element_type=jnp.float32
    ) + lax.dot_general(
        power_weight, power * jnp.bfloat16(-0.5), (((1,), (1,)), ((), ())), preferred_element_type=jnp.float32
    )
    score = score + jnp.take(log_prior, row_class)[None, :]
    best_score = jnp.max(score, axis=1)
    step = 1
    while step < cls_size:
        pairs = [(c, c ^ step) for c in range(cls_size)]
        best_score = jnp.maximum(best_score, lax.ppermute(best_score, "cls", pairs))
        step *= 2

    capacity = max(2, 3 * local_rows // (dom_size * cls_size))
    slots = dom_size * capacity
    fact_class = every_fact[3].astype(jnp.float32).astype(jnp.int32) - dom_index * owned
    owned_here = (fact_class >= 0) & (fact_class < owned)
    running = jnp.cumsum(owned_here.astype(jnp.int32))
    slot_of = jnp.where(owned_here, running - 1, -1)
    slot_ids = jnp.arange(slots, dtype=jnp.int32)
    picker = (slot_ids[:, None] == slot_of[None, :]).astype(jnp.bfloat16)
    picked = lax.dot_general(
        every_fact, picker, (((1,), (1,)), ((), ())), preferred_element_type=jnp.float32
    )
    filled = slot_ids < running[-1]
    slot_defocus = jnp.where(filled, (picked[0] + picked[1]) + picked[2], 1.0)
    slot_pose = picked[3].astype(jnp.int32) - dom_index * owned
    slot_pose = jnp.where(filled, slot_pose * rotations + picked[4].astype(jnp.int32), -1)
    slot_power = power_rows(slot_defocus, inv_noise)
    own_poses = jnp.arange(owned * rotations, dtype=jnp.int32)
    gather_own = (own_poses[:, None] == slot_pose[None, :]).astype(jnp.bfloat16)
    denominator = jnp.dot(gather_own, slot_power, preferred_element_type=jnp.float32)

    class_images = numerator / (jnp.concatenate([denominator, denominator], axis=1) + 1.0)
    return best_score, class_images.reshape(owned, rotations, 2 * pixels)


def solution(mesh):
    dom_size, cls_size = mesh.devices.shape
    split = Mesh(mesh.devices.reshape(dom_size // 2, 2, cls_size), ("chip", "core", "cls"))
    dom = ("chip", "core")
    placed = (P(dom, None), P(dom), P(), P(("cls",) + dom, None, None), P(dom), P(dom), P())
    return jax.shard_map(
        on_device,
        mesh=split,
        in_specs=placed,
        out_specs=(P(dom), P(("cls",) + dom, None, None)),
        check_vma=False,
    )
```

```python
import math

import jax
import jax.numpy as jnp
from jax import lax
from jax.experimental import pallas as pl
from jax.sharding import Mesh, PartitionSpec as P

AMPLITUDE = math.hypot(0.995, 0.1)
PHASE = math.atan2(0.1, 0.995)
ROW_BLOCK = 128


def split_pieces(values, width):
    pieces = []
    rest = values
    for _ in range(3):
        piece = lax.reduce_precision(rest, exponent_bits=8, mantissa_bits=7)
        pieces.append(piece.astype(jnp.bfloat16))
        rest = rest - piece
    joined = jnp.concatenate(pieces, axis=1)
    return jnp.pad(joined, ((0, 0), (0, width - joined.shape[1])))


def contrast_tables(defocus, pixels):
    groups = pixels // 64
    scaled = 12.0 * defocus
    row_offset = (jnp.arange(groups, dtype=jnp.int32) - pixels // 128).astype(jnp.float32)
    row_angle = scaled[:, None] * (row_offset * row_offset / 4096.0)[None, :]
    column = jnp.arange(64, dtype=jnp.int32).astype(jnp.float32)
    column_angle = scaled[:, None] * (column * column / 4096.0)[None, :] + PHASE
    width = -(-3 * groups // 128) * 128
    row_sin = split_pieces(-AMPLITUDE * jnp.sin(row_angle), width)
    row_cos = split_pieces(-AMPLITUDE * jnp.cos(row_angle), width)
    slot = jnp.arange(width, dtype=jnp.int32)[:, None]
    group_of = (jnp.arange(pixels, dtype=jnp.int32) // 64)[None, :]
    expand = ((slot < 3 * groups) & (slot % groups == group_of)).astype(jnp.bfloat16)
    col_cos = jnp.cos(column_angle)
    col_sin = jnp.sin(column_angle)
    return row_sin, row_cos, expand, jnp.concatenate([col_cos, col_cos], 1), jnp.concatenate([col_sin, col_sin], 1)


def contrast_tile(row_sin, row_cos, col_cos, col_sin, tile):
    lanes = slice(tile * 128, (tile + 1) * 128)
    return row_sin[:, lanes] * col_cos + row_cos[:, lanes] * col_sin


def weights_kernel(
    row_sin_ref, row_cos_ref, expand_ref, col_cos_ref, col_sin_ref, noise_ref, particles_ref, selector_ref,
    out_ref, power_ref, sums_ref,
):
    pixels = noise_ref.shape[1]
    row_sin_pieces = row_sin_ref[...]
    row_cos_pieces = row_cos_ref[...]
    col_cos = col_cos_ref[...]
    col_sin = col_sin_ref[...]
    for tile in range(pixels // 128):
        lanes = slice(tile * 128, (tile + 1) * 128)
        imag = slice(pixels + tile * 128, pixels + (tile + 1) * 128)
        expand = expand_ref[:, lanes]
        row_sin = jnp.dot(row_sin_pieces, expand, preferred_element_type=jnp.float32)
        row_cos = jnp.dot(row_cos_pieces, expand, preferred_element_type=jnp.float32)
        contrast_rows = row_sin * col_cos + row_cos * col_sin
        factor = noise_ref[:, lanes] * contrast_rows
        out_ref[:, lanes] = (particles_ref[:, lanes].astype(jnp.float32) * factor).astype(jnp.bfloat16)
        out_ref[:, imag] = (particles_ref[:, imag].astype(jnp.float32) * factor).astype(jnp.bfloat16)
        power_ref[:, lanes] = (factor * contrast_rows).astype(jnp.bfloat16)

    @pl.when(pl.program_id(0) == 0)
    def _():
        sums_ref[...] = jnp.zeros_like(sums_ref)

    sums_ref[...] += jnp.dot(selector_ref[...], out_ref[...], preferred_element_type=jnp.float32)


def power_kernel(row_sin_ref, row_cos_ref, expand_ref, col_cos_ref, col_sin_ref, noise_ref, power_ref):
    pixels = noise_ref.shape[1]
    row_sin = jnp.dot(row_sin_ref[...], expand_ref[...], preferred_element_type=jnp.float32)
    row_cos = jnp.dot(row_cos_ref[...], expand_ref[...], preferred_element_type=jnp.float32)
    col_cos = col_cos_ref[...]
    col_sin = col_sin_ref[...]
    for tile in range(pixels // 128):
        lanes = slice(tile * 128, (tile + 1) * 128)
        contrast_rows = contrast_tile(row_sin, row_cos, col_cos, col_sin, tile)
        factor = noise_ref[:, lanes] * contrast_rows
        power_ref[:, lanes] = (factor * contrast_rows).astype(jnp.bfloat16)


def table_specs(block, width, pixels):
    return [
        pl.BlockSpec((block, width), lambda i: (i, 0)),
        pl.BlockSpec((block, width), lambda i: (i, 0)),
        pl.BlockSpec((width, pixels), lambda i: (0, 0)),
        pl.BlockSpec((block, 128), lambda i: (i, 0)),
        pl.BlockSpec((block, 128), lambda i: (i, 0)),
        pl.BlockSpec((1, pixels), lambda i: (0, 0)),
    ]


def weighted_rows(particles, defocus, inv_noise, selector):
    rows = particles.shape[0]
    poses = selector.shape[0]
    pixels = inv_noise.shape[0]
    block = min(2 * ROW_BLOCK if poses * pixels * 8 <= 16 * 2**20 else ROW_BLOCK, rows)
    tables = contrast_tables(defocus, pixels)
    width = tables[0].shape[1]
    return pl.pallas_call(
        weights_kernel,
        grid=(rows // block,),
        in_specs=table_specs(block, width, pixels)
        + [pl.BlockSpec((block, 2 * pixels), lambda i: (i, 0)), pl.BlockSpec((poses, block), lambda i: (0, i))],
        out_specs=[
            pl.BlockSpec((block, 2 * pixels), lambda i: (i, 0)),
            pl.BlockSpec((block, pixels), lambda i: (i, 0)),
            pl.BlockSpec((poses, 2 * pixels), lambda i: (0, 0)),
        ],
        out_shape=[
            jax.ShapeDtypeStruct((rows, 2 * pixels), jnp.bfloat16),
            jax.ShapeDtypeStruct((rows, pixels), jnp.bfloat16),
            jax.ShapeDtypeStruct((poses, 2 * pixels), jnp.float32),
        ],
    )(*tables, inv_noise[None, :], particles, selector)


def power_rows(defocus, inv_noise):
    rows = defocus.shape[0]
    pixels = inv_noise.shape[0]
    block = min(ROW_BLOCK, rows)
    tables = contrast_tables(defocus, pixels)
    width = tables[0].shape[1]
    return pl.pallas_call(
        power_kernel,
        grid=(rows // block,),
        in_specs=table_specs(block, width, pixels),
        out_specs=pl.BlockSpec((block, pixels), lambda i: (i, 0)),
        out_shape=jax.ShapeDtypeStruct((rows, pixels), jnp.bfloat16),
    )(*tables, inv_noise[None, :])


def on_device(particles, defocus, inv_noise, references, part_class, part_rot, counts):
    local_rows = particles.shape[0]
    pixels = inv_noise.shape[0]
    owned = references.shape[0]
    rotations = references.shape[1]
    chips = lax.axis_size("chip")
    dom_size = 2 * chips
    cls_size = lax.axis_size("cls")
    cls_index = lax.axis_index("cls")
    chip = lax.axis_index("chip")
    core = lax.axis_index("core")
    dom_index = 2 * chip + core
    block_classes = dom_size * owned
    block_first = cls_index * block_classes
    swap = [(0, 1), (1, 0)]

    local_class = part_class - block_first
    facts = split_pieces(defocus[None, :], 3 * local_rows).reshape(3, local_rows)
    block_class = jnp.clip(local_class, -1, block_classes).astype(jnp.bfloat16)
    facts = jnp.concatenate([facts, block_class[None, :], part_rot.astype(jnp.bfloat16)[None, :]], axis=0)
    ref_rows = owned * rotations
    extra_lanes = -(-facts.size // (ref_rows * 128)) * 128
    facts = jnp.pad(facts.reshape(-1), (0, extra_lanes * ref_rows - facts.size))
    sending = jnp.concatenate(
        [references.reshape(ref_rows, 2 * pixels), facts.reshape(ref_rows, extra_lanes)], axis=1
    )
    gathered = lax.all_gather(sending, ("chip", "core"), axis=0, tiled=False)
    flat_images = gathered[:, :, : 2 * pixels].reshape(block_classes * rotations, 2 * pixels)
    every_fact = gathered[:, :, 2 * pixels :].reshape(dom_size, -1)[:, : 5 * local_rows]
    row_class = block_first + jnp.arange(block_classes * rotations, dtype=jnp.int32) // rotations
    every_fact = every_fact.reshape(dom_size, 5, local_rows).transpose(1, 0, 2).reshape(5, dom_size * local_rows)
    real_part = flat_images[:, :pixels].astype(jnp.float32)
    imag_part = flat_images[:, pixels:].astype(jnp.float32)
    power = (real_part * real_part + imag_part * imag_part).astype(jnp.bfloat16)

    in_block = (local_class >= 0) & (local_class < block_classes)
    pose = jnp.where(in_block, local_class * rotations + part_rot, -1)
    poses = jnp.arange(block_classes * rotations, dtype=jnp.int32)
    selector = (poses[:, None] == pose[None, :]).astype(jnp.bfloat16)
    weighted, power_weight, partial = weighted_rows(particles, defocus, inv_noise, selector)
    numerator = lax.psum_scatter(partial, ("chip", "core"), scatter_dimension=0, tiled=True)

    class_total = counts.shape[0]
    log_prior = jnp.log(
        (counts + 1).astype(jnp.float32) / (jnp.sum(counts) + class_total).astype(jnp.float32)
    )
    score = lax.dot_general(
        weighted, flat_images, (((1,), (1,)), ((), ())), preferred_element_type=jnp.float32
    ) + lax.dot_general(
        power_weight, power * jnp.bfloat16(-0.5), (((1,), (1,)), ((), ())), preferred_element_type=jnp.float32
    )
    score = score + jnp.take(log_prior, row_class)[None, :]
    best_score = jnp.max(score, axis=1)
    step = 1
    while step < cls_size:
        pairs = [(c, c ^ step) for c in range(cls_size)]
        best_score = jnp.maximum(best_score, lax.ppermute(best_score, "cls", pairs))
        step *= 2

    capacity = max(2, 3 * local_rows // (dom_size * cls_size))
    slots = dom_size * capacity
    fact_class = every_fact[3].astype(jnp.float32).astype(jnp.int32) - dom_index * owned
    owned_here = (fact_class >= 0) & (fact_class < owned)
    running = jnp.cumsum(owned_here.astype(jnp.int32))
    slot_of = jnp.where(owned_here, running - 1, -1)
    slot_ids = jnp.arange(slots, dtype=jnp.int32)
    picker = (slot_ids[:, None] == slot_of[None, :]).astype(jnp.bfloat16)
    picked = lax.dot_general(
        every_fact, picker, (((1,), (1,)), ((), ())), preferred_element_type=jnp.float32
    )
    filled = slot_ids < running[-1]
    slot_defocus = jnp.where(filled, (picked[0] + picked[1]) + picked[2], 1.0)
    slot_pose = picked[3].astype(jnp.int32) - dom_index * owned
    slot_pose = jnp.where(filled, slot_pose * rotations + picked[4].astype(jnp.int32), -1)
    slot_power = power_rows(slot_defocus, inv_noise)
    own_poses = jnp.arange(owned * rotations, dtype=jnp.int32)
    gather_own = (own_poses[:, None] == slot_pose[None, :]).astype(jnp.bfloat16)
    denominator = jnp.dot(gather_own, slot_power, preferred_element_type=jnp.float32)

    class_images = numerator / (jnp.concatenate([denominator, denominator], axis=1) + 1.0)
    return best_score, class_images.reshape(owned, rotations, 2 * pixels)


def solution(mesh):
    dom_size, cls_size = mesh.devices.shape
    split = Mesh(mesh.devices.reshape(dom_size // 2, 2, cls_size), ("chip", "core", "cls"))
    dom = ("chip", "core")
    placed = (P(dom, None), P(dom), P(), P(("cls",) + dom, None, None), P(dom), P(dom), P())
    return jax.shard_map(
        on_device,
        mesh=split,
        in_specs=placed,
        out_specs=(P(dom), P(("cls",) + dom, None, None)),
        check_vma=False,
    )
```

```python
import math

import jax
import jax.numpy as jnp
from jax import lax
from jax.experimental import pallas as pl
from jax.sharding import Mesh, PartitionSpec as P

AMPLITUDE = math.hypot(0.995, 0.1)
PHASE = math.atan2(0.1, 0.995)
ROW_BLOCK = 128


def split_pieces(values, width):
    pieces = []
    rest = values
    for _ in range(3):
        piece = lax.reduce_precision(rest, exponent_bits=8, mantissa_bits=7)
        pieces.append(piece.astype(jnp.bfloat16))
        rest = rest - piece
    joined = jnp.concatenate(pieces, axis=1)
    return jnp.pad(joined, ((0, 0), (0, width - joined.shape[1])))


def contrast_tables(defocus, pixels):
    groups = pixels // 64
    scaled = 12.0 * defocus
    row_offset = (jnp.arange(groups, dtype=jnp.int32) - pixels // 128).astype(jnp.float32)
    row_angle = scaled[:, None] * (row_offset * row_offset / 4096.0)[None, :]
    column = jnp.arange(64, dtype=jnp.int32).astype(jnp.float32)
    column_angle = scaled[:, None] * (column * column / 4096.0)[None, :] + PHASE
    width = -(-groups // 128) * 128
    pad = ((0, 0), (0, width - groups))
    row_sin = jnp.pad(-AMPLITUDE * jnp.sin(row_angle), pad)
    row_cos = jnp.pad(-AMPLITUDE * jnp.cos(row_angle), pad)
    col_cos = jnp.cos(column_angle)
    col_sin = jnp.sin(column_angle)
    return row_sin, row_cos, jnp.concatenate([col_cos, col_cos], 1), jnp.concatenate([col_sin, col_sin], 1)


def contrast_tile(row_sin_ref, row_cos_ref, col_cos, col_sin, tile):
    first_half = lax.broadcasted_iota(jnp.int32, col_cos.shape, 1) < 64
    row_sin = jnp.where(first_half, row_sin_ref[:, 2 * tile : 2 * tile + 1], row_sin_ref[:, 2 * tile + 1 : 2 * tile + 2])
    row_cos = jnp.where(first_half, row_cos_ref[:, 2 * tile : 2 * tile + 1], row_cos_ref[:, 2 * tile + 1 : 2 * tile + 2])
    return row_sin * col_cos + row_cos * col_sin


def weights_kernel(
    row_sin_ref, row_cos_ref, col_cos_ref, col_sin_ref, noise_ref, particles_ref, selector_ref,
    out_ref, power_ref, sums_ref, mine_ref,
):
    pixels = noise_ref.shape[1]
    col_cos = col_cos_ref[...]
    col_sin = col_sin_ref[...]
    for tile in range(pixels // 128):
        lanes = slice(tile * 128, (tile + 1) * 128)
        imag = slice(pixels + tile * 128, pixels + (tile + 1) * 128)
        contrast_rows = contrast_tile(row_sin_ref, row_cos_ref, col_cos, col_sin, tile)
        factor = noise_ref[:, lanes] * contrast_rows
        out_ref[:, lanes] = (particles_ref[:, lanes].astype(jnp.float32) * factor).astype(jnp.bfloat16)
        out_ref[:, imag] = (particles_ref[:, imag].astype(jnp.float32) * factor).astype(jnp.bfloat16)
        power_ref[:, lanes] = (factor * contrast_rows).astype(jnp.bfloat16)

    @pl.when(pl.program_id(0) == 0)
    def _():
        sums_ref[...] = jnp.zeros_like(sums_ref)
        mine_ref[...] = jnp.zeros_like(mine_ref)

    half = sums_ref.shape[0]
    sums_ref[...] += jnp.dot(selector_ref[:half, :], out_ref[...], preferred_element_type=jnp.float32)
    mine_ref[...] += jnp.dot(selector_ref[half:, :], out_ref[...], preferred_element_type=jnp.float32)


def table_specs(block, width, pixels):
    return [
        pl.BlockSpec((block, width), lambda i: (i, 0)),
        pl.BlockSpec((block, width), lambda i: (i, 0)),
        pl.BlockSpec((block, 128), lambda i: (i, 0)),
        pl.BlockSpec((block, 128), lambda i: (i, 0)),
        pl.BlockSpec((1, pixels), lambda i: (0, 0)),
    ]


def expanded_tables(defocus, pixels):
    groups = pixels // 64
    scaled = 12.0 * defocus
    row_offset = (jnp.arange(groups, dtype=jnp.int32) - pixels // 128).astype(jnp.float32)
    row_angle = scaled[:, None] * (row_offset * row_offset / 4096.0)[None, :]
    column = jnp.arange(64, dtype=jnp.int32).astype(jnp.float32)
    column_angle = scaled[:, None] * (column * column / 4096.0)[None, :] + PHASE
    width = -(-3 * groups // 128) * 128
    row_sin = split_pieces(-AMPLITUDE * jnp.sin(row_angle), width)
    row_cos = split_pieces(-AMPLITUDE * jnp.cos(row_angle), width)
    slot = jnp.arange(width, dtype=jnp.int32)[:, None]
    group_of = (jnp.arange(pixels, dtype=jnp.int32) // 64)[None, :]
    expand = ((slot < 3 * groups) & (slot % groups == group_of)).astype(jnp.bfloat16)
    col_cos = jnp.cos(column_angle)
    col_sin = jnp.sin(column_angle)
    return row_sin, row_cos, expand, jnp.concatenate([col_cos, col_cos], 1), jnp.concatenate([col_sin, col_sin], 1)


def expanded_power_kernel(row_sin_ref, row_cos_ref, expand_ref, col_cos_ref, col_sin_ref, noise_ref, power_ref):
    pixels = noise_ref.shape[1]
    row_sin = jnp.dot(row_sin_ref[...], expand_ref[...], preferred_element_type=jnp.float32)
    row_cos = jnp.dot(row_cos_ref[...], expand_ref[...], preferred_element_type=jnp.float32)
    col_cos = col_cos_ref[...]
    col_sin = col_sin_ref[...]
    for tile in range(pixels // 128):
        lanes = slice(tile * 128, (tile + 1) * 128)
        contrast_rows = row_sin[:, lanes] * col_cos + row_cos[:, lanes] * col_sin
        factor = noise_ref[:, lanes] * contrast_rows
        power_ref[:, lanes] = (factor * contrast_rows).astype(jnp.bfloat16)


def expanded_specs(block, width, pixels):
    return [
        pl.BlockSpec((block, width), lambda i: (i, 0)),
        pl.BlockSpec((block, width), lambda i: (i, 0)),
        pl.BlockSpec((width, pixels), lambda i: (0, 0)),
        pl.BlockSpec((block, 128), lambda i: (i, 0)),
        pl.BlockSpec((block, 128), lambda i: (i, 0)),
        pl.BlockSpec((1, pixels), lambda i: (0, 0)),
    ]


def weighted_rows(particles, defocus, inv_noise, selector):
    rows = particles.shape[0]
    poses = selector.shape[0]
    pixels = inv_noise.shape[0]
    block = min(2 * ROW_BLOCK if poses * pixels * 8 <= 16 * 2**20 else ROW_BLOCK, rows)
    tables = contrast_tables(defocus, pixels)
    width = tables[0].shape[1]
    return pl.pallas_call(
        weights_kernel,
        grid=(rows // block,),
        in_specs=table_specs(block, width, pixels)
        + [pl.BlockSpec((block, 2 * pixels), lambda i: (i, 0)), pl.BlockSpec((poses, block), lambda i: (0, i))],
        out_specs=[
            pl.BlockSpec((block, 2 * pixels), lambda i: (i, 0)),
            pl.BlockSpec((block, pixels), lambda i: (i, 0)),
            pl.BlockSpec((poses // 2, 2 * pixels), lambda i: (0, 0)),
            pl.BlockSpec((poses // 2, 2 * pixels), lambda i: (0, 0)),
        ],
        out_shape=[
            jax.ShapeDtypeStruct((rows, 2 * pixels), jnp.bfloat16),
            jax.ShapeDtypeStruct((rows, pixels), jnp.bfloat16),
            jax.ShapeDtypeStruct((poses // 2, 2 * pixels), jnp.float32),
            jax.ShapeDtypeStruct((poses // 2, 2 * pixels), jnp.float32),
        ],
    )(*tables, inv_noise[None, :], particles, selector)


def power_rows(defocus, inv_noise):
    rows = defocus.shape[0]
    pixels = inv_noise.shape[0]
    block = min(ROW_BLOCK, rows)
    tables = expanded_tables(defocus, pixels)
    width = tables[0].shape[1]
    return pl.pallas_call(
        expanded_power_kernel,
        grid=(rows // block,),
        in_specs=expanded_specs(block, width, pixels),
        out_specs=pl.BlockSpec((block, pixels), lambda i: (i, 0)),
        out_shape=jax.ShapeDtypeStruct((rows, pixels), jnp.bfloat16),
    )(*tables, inv_noise[None, :])


def on_device(particles, defocus, inv_noise, references, part_class, part_rot, counts):
    local_rows = particles.shape[0]
    pixels = inv_noise.shape[0]
    owned = references.shape[0]
    rotations = references.shape[1]
    chips = lax.axis_size("chip")
    dom_size = 2 * chips
    cls_size = lax.axis_size("cls")
    cls_index = lax.axis_index("cls")
    chip = lax.axis_index("chip")
    core = lax.axis_index("core")
    dom_index = 2 * chip + core
    block_classes = dom_size * owned
    block_first = cls_index * block_classes
    swap = [(0, 1), (1, 0)]

    local_class = part_class - block_first
    facts = split_pieces(defocus[None, :], 3 * local_rows).reshape(3, local_rows)
    block_class = jnp.clip(local_class, -1, block_classes).astype(jnp.bfloat16)
    facts = jnp.concatenate([facts, block_class[None, :], part_rot.astype(jnp.bfloat16)[None, :]], axis=0)
    ref_rows = owned * rotations
    extra_lanes = -(-facts.size // (ref_rows * 128)) * 128
    facts = jnp.pad(facts.reshape(-1), (0, extra_lanes * ref_rows - facts.size))
    sending = jnp.concatenate(
        [references.reshape(ref_rows, 2 * pixels), facts.reshape(ref_rows, extra_lanes)], axis=1
    )
    gathered = lax.all_gather(sending, ("chip", "core"), axis=0, tiled=False)
    flat_images = gathered[:, :, : 2 * pixels].reshape(block_classes * rotations, 2 * pixels)
    every_fact = gathered[:, :, 2 * pixels :].reshape(dom_size, -1)[:, : 5 * local_rows]
    row_class = block_first + jnp.arange(block_classes * rotations, dtype=jnp.int32) // rotations
    every_fact = every_fact.reshape(dom_size, 5, local_rows).transpose(1, 0, 2).reshape(5, dom_size * local_rows)
    real_part = flat_images[:, :pixels].astype(jnp.float32)
    imag_part = flat_images[:, pixels:].astype(jnp.float32)
    power = (real_part * real_part + imag_part * imag_part).astype(jnp.bfloat16)

    in_block = (local_class >= 0) & (local_class < block_classes)
    owner = local_class // owned
    mine = (owner % 2 == core).astype(jnp.int32)
    pose = ((mine * chips + owner // 2) * owned + local_class % owned) * rotations + part_rot
    pose = jnp.where(in_block, pose, -1)
    poses = jnp.arange(block_classes * rotations, dtype=jnp.int32)
    selector = (poses[:, None] == pose[None, :]).astype(jnp.bfloat16)
    weighted, power_weight, for_other, for_me = weighted_rows(particles, defocus, inv_noise, selector)
    chip_sums = for_me + lax.ppermute(for_other, "core", swap)
    numerator = lax.psum_scatter(chip_sums, "chip", scatter_dimension=0, tiled=True)

    class_total = counts.shape[0]
    log_prior = jnp.log(
        (counts + 1).astype(jnp.float32) / (jnp.sum(counts) + class_total).astype(jnp.float32)
    )
    score = lax.dot_general(
        weighted, flat_images, (((1,), (1,)), ((), ())), preferred_element_type=jnp.float32
    ) + lax.dot_general(
        power_weight, power * jnp.bfloat16(-0.5), (((1,), (1,)), ((), ())), preferred_element_type=jnp.float32
    )
    score = score + jnp.take(log_prior, row_class)[None, :]
    best_score = jnp.max(score, axis=1)
    step = 1
    while step < cls_size:
        pairs = [(c, c ^ step) for c in range(cls_size)]
        best_score = jnp.maximum(best_score, lax.ppermute(best_score, "cls", pairs))
        step *= 2

    capacity = max(2, 3 * local_rows // (dom_size * cls_size))
    slots = dom_size * capacity
    fact_class = every_fact[3].astype(jnp.float32).astype(jnp.int32) - dom_index * owned
    owned_here = (fact_class >= 0) & (fact_class < owned)
    running = jnp.cumsum(owned_here.astype(jnp.int32))
    slot_of = jnp.where(owned_here, running - 1, -1)
    slot_ids = jnp.arange(slots, dtype=jnp.int32)
    picker = (slot_ids[:, None] == slot_of[None, :]).astype(jnp.bfloat16)
    picked = lax.dot_general(
        every_fact, picker, (((1,), (1,)), ((), ())), preferred_element_type=jnp.float32
    )
    filled = slot_ids < running[-1]
    slot_defocus = jnp.where(filled, (picked[0] + picked[1]) + picked[2], 1.0)
    slot_pose = picked[3].astype(jnp.int32) - dom_index * owned
    slot_pose = jnp.where(filled, slot_pose * rotations + picked[4].astype(jnp.int32), -1)
    slot_power = power_rows(slot_defocus, inv_noise)
    own_poses = jnp.arange(owned * rotations, dtype=jnp.int32)
    gather_own = (own_poses[:, None] == slot_pose[None, :]).astype(jnp.bfloat16)
    denominator = jnp.dot(gather_own, slot_power, preferred_element_type=jnp.float32)

    class_images = numerator / (jnp.concatenate([denominator, denominator], axis=1) + 1.0)
    return best_score, class_images.reshape(owned, rotations, 2 * pixels)


def solution(mesh):
    dom_size, cls_size = mesh.devices.shape
    split = Mesh(mesh.devices.reshape(dom_size // 2, 2, cls_size), ("chip", "core", "cls"))
    dom = ("chip", "core")
    placed = (P(dom, None), P(dom), P(), P(("cls",) + dom, None, None), P(dom), P(dom), P())
    return jax.shard_map(
        on_device,
        mesh=split,
        in_specs=placed,
        out_specs=(P(dom), P(("cls",) + dom, None, None)),
        check_vma=False,
    )
```
